256 devices in a mesh: dp: 8 (over x, z_lo), seq: 32 (over z_hi, y, core).
Axes of the slice: x: 4, y: 4, z: 8 (z_hi: 4, z_lo: 2; z = z_hi * 2 + z_lo), core: 2. Of those that a mesh axis runs over, the one named last changes fastest.
Arguments:
- inputs: float32 [8, 4096, 2048], P('dp', 'seq'), may hold values from -6 to 6
- cotangent: float32 [8, 4096, 2048], P('dp', 'seq'), may hold values from -6 to 6
- block_mix: float32 [128, 128], replicated, may hold values from -0.5 to 0.5
- twist_hi: float32 [2, 2, 2048], replicated, may hold values from -3 to 3
- twist_lo: float32 [2, 2, 2048], replicated, may hold values from -3 to 3
- gain: float32 [2048], replicated, may hold values from 0.5 to 1.5
- gate_up: float32 [128, 2, 16, 256], P('seq'), may hold values from -0.5 to 0.5
- down: float32 [256, 16, 128], P('seq'), may hold values from -0.375 to 0.375
Outputs:
- grad_inputs: float32 [8, 4096, 2048], P('dp', 'seq')
- grad_gate_up: float32 [128, 2, 16, 256], P('seq')
- grad_down: float32 [256, 16, 128], P('seq')
- grad_block_mix: float32 [128, 128], replicated
- grad_twist_hi: float32 [2, 2, 2048], replicated
- grad_twist_lo: float32 [2, 2, 2048], replicated
- grad_gain: float32 [2048], replicated
The draws below stay inside these ranges and needn't reach their ends.
All inputs are finite; a program needn't handle non-finite values.
Results may differ from the reference program's by a relative error of at most 0.00022.
Values sent between devices are 32-bit elements; how exact they have to be, the bound alone decides.
No kernel may reach another device: no remote copies, remote signals or barrier semaphores. Data moves between devices by JAX's collectives and lax.ppermute only.
A program may use at most 64 MiB of HBM per device.

```python
import math
import jax
import jax.numpy as jnp
from jax import lax

D = 2048
NB = 16
BLK = 128
TOK_DEV = 128
SHARDS = 32
SEQ_LEN = 4096
SEQS = 8
TOTAL = 32768
DB = 128
FB = 256


def steps_of(key, dims, pieces, least, high):
    factor_of = 1.0
    for dim, shards_of in pieces:
        steps = jax.random.uniform(jax.random.fold_in(jax.random.fold_in(key, 6), dim), (shards_of,), jnp.float32, least / len(pieces), high / len(pieces))
        factor_of = factor_of * jnp.repeat(jnp.exp(steps), dims[dim] // shards_of).reshape((-1,) + (1,) * (len(dims) - 1 - dim))
    return factor_of


def gaussian(own_key, shape, width, limit, split=(), kind=jnp.bfloat16):
    array = jax.random.normal(own_key, shape, jnp.float32) * width
    if len(split) > 0:
        array = steps_of(own_key, shape, split, -0.22, 0.18) * array
    return jnp.clip(array, min=-limit, max=limit).astype(kind)


def setup_inputs(seed: int = 0) -> dict:
    seeds = jax.random.split(jax.random.key(seed), 9)
    return {
        "inputs": gaussian(seeds[0], (SEQS, SEQ_LEN, D), 1.0, 6.0, ((0, 8), (1, 32)), jnp.float32),
        "cotangent": gaussian(seeds[1], (SEQS, SEQ_LEN, D), 1.0, 6.0, ((0, 8), (1, 32)), jnp.float32),
        "block_mix": gaussian(seeds[2], (BLK, BLK), BLK ** -0.5, 0.5, (), jnp.float32),
        "twist_hi": gaussian(seeds[3], (2, 2, D), 0.7, 3.0, (), jnp.float32),
        "twist_lo": gaussian(seeds[4], (2, 2, D), 0.7, 3.0, (), jnp.float32),
        "gain": jnp.clip(1.0 + 0.1 * jax.random.normal(seeds[5], (D,), jnp.float32), 0.5, 1.5),
        "gate_up": gaussian(seeds[6], (DB, 2, NB, FB), DB ** -0.5, 0.5, ((0, 32),), jnp.float32),
        "down": gaussian(seeds[7], (FB, NB, DB), FB ** -0.5, 0.375, ((0, 32),), jnp.float32),
    }


HIGH = lax.Precision.HIGHEST
EPS = 1e-05

def section(field, coeff, distance):
    blocks = field.reshape(SHARDS, TOK_DEV, D)
    index = jnp.arange(SHARDS, dtype=jnp.int32)
    side = index // distance % 2
    partner = index + distance - 2 * distance * side
    own = coeff[side]
    result = own[:, 0][:, None, :] * blocks + own[:, 1][:, None, :] * blocks[partner]
    return result.reshape(SEQ_LEN, D)

def forward(seq_in, block_mix, twist_hi, twist_lo, gain, gate_up, down):
    xb = seq_in.reshape(SEQ_LEN // BLK, BLK, D)
    mixed = jnp.einsum('ij,kjd->kid', block_mix, xb, precision=HIGH).reshape(SEQ_LEN, D)
    first = section(mixed, twist_hi, SHARDS // 2)
    second = section(first, twist_lo, 1)
    resid = seq_in + second
    scale = lax.rsqrt(lax.optimization_barrier(jnp.mean(resid * resid, axis=-1, keepdims=True)) + EPS)
    normed = (resid * scale * gain).reshape(SEQ_LEN, NB, DB)
    gate_val = jnp.einsum('tnd,dnf->tnf', normed, gate_up[:, 0], precision=HIGH)
    up_val = jnp.einsum('tnd,dnf->tnf', normed, gate_up[:, 1], precision=HIGH)
    hidden = jax.nn.silu(gate_val) * up_val
    projected = jnp.einsum('tnf,fnd->tnd', hidden, down, precision=HIGH).reshape(SEQ_LEN, D)
    return resid + projected

def reference(inputs, cotangent, block_mix, twist_hi, twist_lo, gain, gate_up, down):
    params = (block_mix, twist_hi, twist_lo, gain, gate_up, down)

    def one_sequence(carry, pair):
        seq_in, seq_cot = pair
        _, pull = jax.vjp(forward, seq_in, *params)
        grads = pull(seq_cot)
        carry = tuple((c + g for c, g in zip(carry, grads[1:])))
        return (carry, grads[0])
    start = tuple((jnp.zeros(p.shape, jnp.float32) for p in params))
    totals, grad_inputs = lax.scan(one_sequence, start, (inputs, cotangent))
    factor = 1.0 / math.sqrt(TOTAL)
    g_block, g_hi, g_lo, g_gain, g_gu, g_down = [t * factor for t in totals]
    return (grad_inputs, g_gu, g_down, g_block, g_hi, g_lo, g_gain)
```

```python
import math

import jax
import jax.numpy as jnp
from jax import lax
from jax.sharding import PartitionSpec as P

NB = 16
BLK = 128
DB = 128


HIGH = lax.Precision.HIGHEST
EPS = 1e-05


def from_partner(block, axis, distance):
    count = lax.axis_size(axis)
    route = []
    for low in range(count):
        high = low | 1 << distance
        if high != low and high < count:
            route += [(low, high), (high, low)]
    return lax.ppermute(block, axis, route)


def side_of(bit):
    return lax.axis_index("seq") // (1 << bit) % 2


def forward_section(field, coeff, bit):
    partner = from_partner(field, "seq", bit)
    own = coeff[side_of(bit)]
    return (own[0] * field + own[1] * partner, partner)


def backward_section(grad, field, partner, coeff, bit):
    side = side_of(bit)
    own = coeff[side]
    sent = from_partner(own[1] * grad, "seq", bit)
    back = own[0] * grad + sent
    term = jnp.stack([jnp.sum(grad * field, axis=0), jnp.sum(grad * partner, axis=0)])
    pick = (jnp.arange(2) == side).astype(jnp.float32)
    return (back, pick[:, None, None] * term[None])


def exchange(x):
    return lax.all_to_all(x, "seq", 0, 0, tiled=True)


def to_blocks(field, count):
    tokens = field.shape[0]
    halves = count // NB
    x = field.reshape(halves, tokens // halves, NB, DB)
    x = jnp.transpose(x, (2, 0, 1, 3))
    return x.reshape(count, tokens // halves, DB)


def from_blocks(x, tokens, count):
    halves = count // NB
    x = x.reshape(NB, halves, tokens // halves, DB)
    x = jnp.transpose(x, (1, 2, 0, 3))
    return x.reshape(tokens, NB * DB)


def per_device(inputs, cotangent, block_mix, twist_hi, twist_lo, gain, gate_up, down):
    seq_in = inputs[0]
    tokens, width = seq_in.shape
    count = lax.axis_size("seq")
    halves = count // NB
    top_bit = count.bit_length() - 2
    nblocks = tokens // BLK
    rows_gu = gate_up.shape[0]
    rows_dn = down.shape[0]
    fb = gate_up.shape[3]

    gu_n = jnp.transpose(gate_up, (2, 0, 1, 3)).reshape(NB, rows_gu * 2 * fb)
    dn_n = jnp.transpose(down, (1, 0, 2)).reshape(NB, rows_dn * DB)
    wbuf = jnp.concatenate([gu_n, dn_n], axis=1)
    wbuf = jnp.repeat(wbuf, halves, axis=0)
    wrecv = exchange(wbuf)
    w_gu = wrecv[:, : rows_gu * 2 * fb].reshape(count * rows_gu, 2, fb)
    w_dn = wrecv[:, rows_gu * 2 * fb :].reshape(count * rows_dn, DB)

    grad_out = cotangent[0]
    cot_blk = exchange(to_blocks(grad_out, count)).reshape(-1, DB)

    xb = seq_in.reshape(nblocks, BLK, width)
    mixed = jnp.einsum("ij,kjd->kid", block_mix, xb, precision=HIGH).reshape(tokens, width)
    first, mixed_peer = forward_section(mixed, twist_hi, top_bit)
    second, first_peer = forward_section(first, twist_lo, 0)
    resid = seq_in + second
    scale = lax.rsqrt(jnp.mean(resid * resid, axis=-1, keepdims=True) + EPS)
    unit = resid * scale
    normed = unit * gain
    x_blk = exchange(to_blocks(normed, count)).reshape(-1, DB)

    gate_val = jnp.dot(x_blk, w_gu[:, 0], precision=HIGH)
    up_val = jnp.dot(x_blk, w_gu[:, 1], precision=HIGH)
    sig = jax.nn.sigmoid(gate_val)
    act = gate_val * sig
    hidden = act * up_val
    grad_hidden = jnp.dot(cot_blk, w_dn.T, precision=HIGH)
    grad_gate = grad_hidden * up_val * sig * (1.0 + gate_val * (1.0 - sig))
    grad_up = grad_hidden * act
    grad_x = jnp.dot(grad_gate, w_gu[:, 0].T, precision=HIGH) + jnp.dot(grad_up, w_gu[:, 1].T, precision=HIGH)
    grad_normed = from_blocks(exchange(grad_x.reshape(count, -1, DB)), tokens, count)

    d_gate = jnp.dot(x_blk.T, grad_gate, precision=HIGH)
    d_up = jnp.dot(x_blk.T, grad_up, precision=HIGH)
    d_gu = jnp.stack([d_gate, d_up], axis=1).reshape(count, rows_gu * 2 * fb)
    d_dn = jnp.dot(hidden.T, cot_blk, precision=HIGH).reshape(count, rows_dn * DB)
    grecv = exchange(jnp.concatenate([d_gu, d_dn], axis=1))
    grecv = grecv.reshape(NB, halves, -1).sum(axis=1)
    part_gu = jnp.transpose(grecv[:, : rows_gu * 2 * fb].reshape(NB, rows_gu, 2, fb), (1, 2, 0, 3))
    part_down = jnp.transpose(grecv[:, rows_gu * 2 * fb :].reshape(NB, rows_dn, DB), (1, 0, 2))
    part_gu, part_down = lax.psum((part_gu, part_down), "dp")

    grad_gain_local = jnp.sum(grad_normed * unit, axis=0)
    weighted = grad_normed * gain
    inner = jnp.mean(weighted * resid, axis=-1, keepdims=True)
    grad_resid = grad_out + scale * weighted - resid * scale * scale * scale * inner
    grad_first, term_lo = backward_section(grad_resid, first, first_peer, twist_lo, 0)
    grad_mixed, term_hi = backward_section(grad_first, mixed, mixed_peer, twist_hi, top_bit)
    grad_mb = grad_mixed.reshape(nblocks, BLK, width)
    term_block = jnp.einsum("kid,kjd->ij", grad_mb, xb, precision=HIGH)
    grad_seq = jnp.einsum("ij,kid->kjd", block_mix, grad_mb, precision=HIGH).reshape(tokens, width)
    grad_seq = grad_seq + grad_resid
    sum_block, sum_hi, sum_lo, sum_gain = lax.psum(
        (term_block, term_hi, term_lo, grad_gain_local), ("dp", "seq")
    )
    factor = 1.0 / math.sqrt(lax.axis_size("dp") * count * tokens)
    return (
        grad_seq[None],
        part_gu * factor,
        part_down * factor,
        sum_block * factor,
        sum_hi * factor,
        sum_lo * factor,
        sum_gain * factor,
    )


def solution(mesh):
    return jax.shard_map(
        per_device,
        mesh=mesh,
        in_specs=(
            P("dp", "seq", None),
            P("dp", "seq", None),
            P(),
            P(),
            P(),
            P(),
            P("seq", None, None, None),
            P("seq", None, None),
        ),
        out_specs=(
            P("dp", "seq", None),
            P("seq", None, None, None),
            P("seq", None, None),
            P(),
            P(),
            P(),
            P(),
        ),
        check_vma=False,
    )
```

```python
import math

import jax
import jax.numpy as jnp
from jax import lax
from jax.sharding import PartitionSpec as P

NB = 16
BLK = 128
DB = 128


HIGH = lax.Precision.HIGHEST
EPS = 1e-05


def from_partner(block, axis, distance):
    count = lax.axis_size(axis)
    route = []
    for low in range(count):
        high = low | 1 << distance
        if high != low and high < count:
            route += [(low, high), (high, low)]
    return lax.ppermute(block, axis, route)


def side_of(bit):
    return lax.axis_index("seq") // (1 << bit) % 2


def forward_section(field, coeff, bit):
    partner = from_partner(field, "seq", bit)
    own = coeff[side_of(bit)]
    return (own[0] * field + own[1] * partner, partner)


def backward_section(grad, field, partner, coeff, bit):
    side = side_of(bit)
    own = coeff[side]
    sent = from_partner(own[1] * grad, "seq", bit)
    back = own[0] * grad + sent
    term = jnp.stack([jnp.sum(grad * field, axis=0), jnp.sum(grad * partner, axis=0)])
    pick = (jnp.arange(2) == side).astype(jnp.float32)
    return (back, pick[:, None, None] * term[None])


def psum_doubling(x, axis):
    for bit in range(lax.axis_size(axis).bit_length() - 1):
        x = x + from_partner(x, axis, bit)
    return x


def exchange(x):
    return lax.all_to_all(x, "seq", 0, 0, tiled=True)


def to_blocks(field, count):
    tokens = field.shape[0]
    halves = count // NB
    x = field.reshape(halves, tokens // halves, NB, DB)
    x = jnp.transpose(x, (2, 0, 1, 3))
    return x.reshape(count, tokens // halves, DB)


def from_blocks(x, tokens, count):
    halves = count // NB
    x = x.reshape(NB, halves, tokens // halves, DB)
    x = jnp.transpose(x, (1, 2, 0, 3))
    return x.reshape(tokens, NB * DB)


def per_device(inputs, cotangent, block_mix, twist_hi, twist_lo, gain, gate_up, down):
    seq_in = inputs[0]
    tokens, width = seq_in.shape
    count = lax.axis_size("seq")
    halves = count // NB
    top_bit = count.bit_length() - 2
    nblocks = tokens // BLK
    rows_gu = gate_up.shape[0]
    rows_dn = down.shape[0]
    fb = gate_up.shape[3]

    gu_n = jnp.transpose(gate_up, (2, 0, 1, 3)).reshape(NB, rows_gu * 2 * fb)
    dn_n = jnp.transpose(down, (1, 0, 2)).reshape(NB, rows_dn * DB)
    wbuf = jnp.concatenate([gu_n, dn_n], axis=1)
    wbuf = jnp.repeat(wbuf, halves, axis=0)
    wrecv = exchange(wbuf)
    w_gu = wrecv[:, : rows_gu * 2 * fb].reshape(count * rows_gu, 2, fb)
    w_dn = wrecv[:, rows_gu * 2 * fb :].reshape(count * rows_dn, DB)

    grad_out = cotangent[0]
    cot_blk = exchange(to_blocks(grad_out, count)).reshape(-1, DB)

    xb = seq_in.reshape(nblocks, BLK, width)
    mixed = jnp.einsum("ij,kjd->kid", block_mix, xb, precision=HIGH).reshape(tokens, width)
    first, mixed_peer = forward_section(mixed, twist_hi, top_bit)
    second, first_peer = forward_section(first, twist_lo, 0)
    resid = seq_in + second
    scale = lax.rsqrt(jnp.mean(resid * resid, axis=-1, keepdims=True) + EPS)
    unit = resid * scale
    normed = unit * gain
    x_blk = exchange(to_blocks(normed, count)).reshape(-1, DB)

    gate_val = jnp.dot(x_blk, w_gu[:, 0], precision=HIGH)
    up_val = jnp.dot(x_blk, w_gu[:, 1], precision=HIGH)
    sig = jax.nn.sigmoid(gate_val)
    act = gate_val * sig
    hidden = act * up_val
    grad_hidden = jnp.dot(cot_blk, w_dn.T, precision=HIGH)
    grad_gate = grad_hidden * up_val * sig * (1.0 + gate_val * (1.0 - sig))
    grad_up = grad_hidden * act
    grad_x = jnp.dot(grad_gate, w_gu[:, 0].T, precision=HIGH) + jnp.dot(grad_up, w_gu[:, 1].T, precision=HIGH)
    grad_normed = from_blocks(exchange(grad_x.reshape(count, -1, DB)), tokens, count)

    d_gate = jnp.dot(x_blk.T, grad_gate, precision=HIGH)
    d_up = jnp.dot(x_blk.T, grad_up, precision=HIGH)
    d_gu = jnp.stack([d_gate, d_up], axis=1).reshape(count, rows_gu * 2 * fb)
    d_dn = jnp.dot(hidden.T, cot_blk, precision=HIGH).reshape(count, rows_dn * DB)
    grecv = exchange(jnp.concatenate([d_gu, d_dn], axis=1))
    grecv = grecv.reshape(NB, halves, -1).sum(axis=1)
    part_gu = jnp.transpose(grecv[:, : rows_gu * 2 * fb].reshape(NB, rows_gu, 2, fb), (1, 2, 0, 3))
    part_down = jnp.transpose(grecv[:, rows_gu * 2 * fb :].reshape(NB, rows_dn, DB), (1, 0, 2))
    n_gu = part_gu.size
    wsum = psum_doubling(jnp.concatenate([part_gu.reshape(-1), part_down.reshape(-1)]), "dp")
    part_gu = wsum[:n_gu].reshape(part_gu.shape)
    part_down = wsum[n_gu:].reshape(part_down.shape)

    grad_gain_local = jnp.sum(grad_normed * unit, axis=0)
    weighted = grad_normed * gain
    inner = jnp.mean(weighted * resid, axis=-1, keepdims=True)
    grad_resid = grad_out + scale * weighted - resid * scale * scale * scale * inner
    grad_first, term_lo = backward_section(grad_resid, first, first_peer, twist_lo, 0)
    grad_mixed, term_hi = backward_section(grad_first, mixed, mixed_peer, twist_hi, top_bit)
    grad_mb = grad_mixed.reshape(nblocks, BLK, width)
    term_block = jnp.einsum("kid,kjd->ij", grad_mb, xb, precision=HIGH)
    grad_seq = jnp.einsum("ij,kid->kjd", block_mix, grad_mb, precision=HIGH).reshape(tokens, width)
    grad_seq = grad_seq + grad_resid
    smalls = (term_block, term_hi, term_lo, grad_gain_local)
    sbuf = jnp.concatenate([t.reshape(-1) for t in smalls])
    spart = exchange(sbuf.reshape(count, -1)).sum(axis=0)
    spart = psum_doubling(spart, "dp")
    sfull = exchange(jnp.broadcast_to(spart[None], (count, spart.shape[0]))).reshape(-1)
    sums = []
    at = 0
    for t in smalls:
        sums.append(sfull[at : at + t.size].reshape(t.shape))
        at += t.size
    sum_block, sum_hi, sum_lo, sum_gain = sums
    factor = 1.0 / math.sqrt(lax.axis_size("dp") * count * tokens)
    return (
        grad_seq[None],
        part_gu * factor,
        part_down * factor,
        sum_block * factor,
        sum_hi * factor,
        sum_lo * factor,
        sum_gain * factor,
    )


def solution(mesh):
    return jax.shard_map(
        per_device,
        mesh=mesh,
        in_specs=(
            P("dp", "seq", None),
            P("dp", "seq", None),
            P(),
            P(),
            P(),
            P(),
            P("seq", None, None, None),
            P("seq", None, None),
        ),
        out_specs=(
            P("dp", "seq", None),
            P("seq", None, None, None),
            P("seq", None, None),
            P(),
            P(),
            P(),
            P(),
        ),
        check_vma=False,
    )
```

```python
import math

import jax
import jax.numpy as jnp
from jax import lax
from jax.sharding import PartitionSpec as P

NB = 16
BLK = 128
DB = 128


HIGH = lax.Precision.HIGHEST
EPS = 1e-05


def from_partner(block, axis, distance):
    count = lax.axis_size(axis)
    route = []
    for low in range(count):
        high = low | 1 << distance
        if high != low and high < count:
            route += [(low, high), (high, low)]
    return lax.ppermute(block, axis, route)


def side_of(bit):
    return lax.axis_index("seq") // (1 << bit) % 2


def forward_section(field, coeff, bit):
    partner = from_partner(field, "seq", bit)
    own = coeff[side_of(bit)]
    return (own[0] * field + own[1] * partner, partner)


def backward_section(grad, field, partner, coeff, bit):
    side = side_of(bit)
    own = coeff[side]
    sent = from_partner(own[1] * grad, "seq", bit)
    back = own[0] * grad + sent
    term = jnp.stack([jnp.sum(grad * field, axis=0), jnp.sum(grad * partner, axis=0)])
    pick = (jnp.arange(2) == side).astype(jnp.float32)
    return (back, pick[:, None, None] * term[None])


def psum_doubling(x, axis):
    for bit in range(lax.axis_size(axis).bit_length() - 1):
        x = x + from_partner(x, axis, bit)
    return x


def exchange(x):
    return lax.all_to_all(x, "seq", 0, 0, tiled=True)


def to_blocks(field, count):
    tokens = field.shape[0]
    halves = count // NB
    x = field.reshape(halves, tokens // halves, NB, DB)
    x = jnp.transpose(x, (2, 0, 1, 3))
    return x.reshape(count, tokens // halves, DB)


def from_blocks(x, tokens, count):
    halves = count // NB
    x = x.reshape(NB, halves, tokens // halves, DB)
    x = jnp.transpose(x, (1, 2, 0, 3))
    return x.reshape(tokens, NB * DB)


def per_device(inputs, cotangent, block_mix, twist_hi, twist_lo, gain, gate_up, down):
    seq_in = inputs[0]
    tokens, width = seq_in.shape
    count = lax.axis_size("seq")
    halves = count // NB
    top_bit = count.bit_length() - 2
    nblocks = tokens // BLK
    rows_gu = gate_up.shape[0]
    rows_dn = down.shape[0]
    fb = gate_up.shape[3]

    gu_n = jnp.transpose(gate_up, (2, 0, 1, 3)).reshape(NB, rows_gu * 2 * fb)
    dn_n = jnp.transpose(down, (1, 0, 2)).reshape(NB, rows_dn * DB)
    wbuf = jnp.concatenate([gu_n, dn_n], axis=1)
    wbuf = jnp.repeat(wbuf, halves, axis=0)
    wrecv = exchange(wbuf)
    w_gu = wrecv[:, : rows_gu * 2 * fb].reshape(count * rows_gu, 2, fb)
    w_dn = wrecv[:, rows_gu * 2 * fb :].reshape(count * rows_dn, DB)

    grad_out = cotangent[0]
    cot_blk = exchange(to_blocks(grad_out, count)).reshape(-1, DB)

    xb = seq_in.reshape(nblocks, BLK, width)
    xb_peer = from_partner(xb, "seq", top_bit)
    mixed = jnp.einsum("ij,kjd->kid", block_mix, xb, precision=HIGH).reshape(tokens, width)
    mixed_peer = jnp.einsum("ij,kjd->kid", block_mix, xb_peer, precision=HIGH).reshape(tokens, width)
    own_hi = twist_hi[side_of(top_bit)]
    first = own_hi[0] * mixed + own_hi[1] * mixed_peer
    second, first_peer = forward_section(first, twist_lo, 0)
    resid = seq_in + second
    scale = lax.rsqrt(jnp.mean(resid * resid, axis=-1, keepdims=True) + EPS)
    unit = resid * scale
    normed = unit * gain
    x_blk = exchange(to_blocks(normed, count)).reshape(-1, DB)

    gate_val = jnp.dot(x_blk, w_gu[:, 0], precision=HIGH)
    up_val = jnp.dot(x_blk, w_gu[:, 1], precision=HIGH)
    sig = jax.nn.sigmoid(gate_val)
    act = gate_val * sig
    hidden = act * up_val
    grad_hidden = jnp.dot(cot_blk, w_dn.T, precision=HIGH)
    grad_gate = grad_hidden * up_val * sig * (1.0 + gate_val * (1.0 - sig))
    grad_up = grad_hidden * act
    grad_x = jnp.dot(grad_gate, w_gu[:, 0].T, precision=HIGH) + jnp.dot(grad_up, w_gu[:, 1].T, precision=HIGH)
    grad_normed = from_blocks(exchange(grad_x.reshape(count, -1, DB)), tokens, count)

    d_gate = jnp.dot(x_blk.T, grad_gate, precision=HIGH)
    d_up = jnp.dot(x_blk.T, grad_up, precision=HIGH)
    d_gu = jnp.stack([d_gate, d_up], axis=1).reshape(count, rows_gu * 2 * fb)
    d_dn = jnp.dot(hidden.T, cot_blk, precision=HIGH).reshape(count, rows_dn * DB)
    grecv = exchange(jnp.concatenate([d_gu, d_dn], axis=1))
    grecv = grecv.reshape(NB, halves, -1).sum(axis=1)
    part_gu = jnp.transpose(grecv[:, : rows_gu * 2 * fb].reshape(NB, rows_gu, 2, fb), (1, 2, 0, 3))
    part_down = jnp.transpose(grecv[:, rows_gu * 2 * fb :].reshape(NB, rows_dn, DB), (1, 0, 2))
    n_gu = part_gu.size
    wsum = psum_doubling(jnp.concatenate([part_gu.reshape(-1), part_down.reshape(-1)]), "dp")
    part_gu = wsum[:n_gu].reshape(part_gu.shape)
    part_down = wsum[n_gu:].reshape(part_down.shape)

    grad_gain_local = jnp.sum(grad_normed * unit, axis=0)
    weighted = grad_normed * gain
    inner = jnp.mean(weighted * resid, axis=-1, keepdims=True)
    grad_resid = grad_out + scale * weighted - resid * scale * scale * scale * inner
    grad_first, term_lo = backward_section(grad_resid, first, first_peer, twist_lo, 0)
    grad_mixed, term_hi = backward_section(grad_first, mixed, mixed_peer, twist_hi, top_bit)
    grad_mb = grad_mixed.reshape(nblocks, BLK, width)
    keep = (own_hi[0] * grad_first).reshape(nblocks, BLK, width)
    give = (own_hi[1] * grad_first).reshape(nblocks, BLK, width)
    term_block = jnp.einsum("kid,kjd->ij", keep, xb, precision=HIGH) + jnp.einsum(
        "kid,kjd->ij", give, xb_peer, precision=HIGH
    )
    grad_seq = jnp.einsum("ij,kid->kjd", block_mix, grad_mb, precision=HIGH).reshape(tokens, width)
    grad_seq = grad_seq + grad_resid
    smalls = (term_block, term_hi, term_lo, grad_gain_local)
    sbuf = jnp.concatenate([t.reshape(-1) for t in smalls])
    spart = exchange(sbuf.reshape(count, -1)).sum(axis=0)
    spart = psum_doubling(spart, "dp")
    sfull = exchange(jnp.broadcast_to(spart[None], (count, spart.shape[0]))).reshape(-1)
    sums = []
    at = 0
    for t in smalls:
        sums.append(sfull[at : at + t.size].reshape(t.shape))
        at += t.size
    sum_block, sum_hi, sum_lo, sum_gain = sums
    factor = 1.0 / math.sqrt(lax.axis_size("dp") * count * tokens)
    return (
        grad_seq[None],
        part_gu * factor,
        part_down * factor,
        sum_block * factor,
        sum_hi * factor,
        sum_lo * factor,
        sum_gain * factor,
    )


def solution(mesh):
    return jax.shard_map(
        per_device,
        mesh=mesh,
        in_specs=(
            P("dp", "seq", None),
            P("dp", "seq", None),
            P(),
            P(),
            P(),
            P(),
            P("seq", None, None, None),
            P("seq", None, None),
        ),
        out_specs=(
            P("dp", "seq", None),
            P("seq", None, None, None),
            P("seq", None, None),
            P(),
            P(),
            P(),
            P(),
        ),
        check_vma=False,
    )
```

```python
import math

import jax
import jax.numpy as jnp
from jax import lax
from jax.sharding import Mesh, PartitionSpec as P

NB = 16
BLK = 128
DB = 128


HIGH = lax.Precision.HIGHEST
EPS = 1e-05


def axis_count(axis):
    if isinstance(axis, tuple):
        return math.prod(lax.axis_size(a) for a in axis)
    return lax.axis_size(axis)


def from_partner(block, axis, distance):
    count = axis_count(axis)
    route = []
    for low in range(count):
        high = low | 1 << distance
        if high != low and high < count:
            route += [(low, high), (high, low)]
    return lax.ppermute(block, axis, route)


SEQ = ("zh", "loc")


def side_of(bit):
    return lax.axis_index(SEQ) // (1 << bit) % 2


def forward_section(field, coeff, bit):
    partner = from_partner(field, SEQ, bit)
    own = coeff[side_of(bit)]
    return (own[0] * field + own[1] * partner, partner)


def backward_section(grad, field, partner, coeff, bit):
    side = side_of(bit)
    own = coeff[side]
    sent = from_partner(own[1] * grad, SEQ, bit)
    back = own[0] * grad + sent
    term = jnp.stack([jnp.sum(grad * field, axis=0), jnp.sum(grad * partner, axis=0)])
    pick = (jnp.arange(2) == side).astype(jnp.float32)
    return (back, pick[:, None, None] * term[None])


def psum_doubling(x, axis):
    for bit in range(axis_count(axis).bit_length() - 1):
        x = x + from_partner(x, axis, bit)
    return x


def exchange(x, axis=SEQ):
    return lax.all_to_all(x, axis, 0, 0, tiled=True)


def per_device(inputs, cotangent, block_mix, twist_hi, twist_lo, gain, gate_up, down):
    seq_in = inputs[0]
    tokens, width = seq_in.shape
    count = axis_count(SEQ)
    group = lax.axis_size("loc")
    zcount = count // group
    nb = NB // group
    top_bit = count.bit_length() - 2
    nblocks = tokens // BLK
    rows_gu = gate_up.shape[0]
    rows_dn = down.shape[0]
    fb = gate_up.shape[3]
    size_gu = rows_gu * 2 * nb * fb

    gu_l = jnp.transpose(gate_up.reshape(rows_gu, 2, group, nb, fb), (2, 0, 1, 3, 4)).reshape(group, -1)
    dn_l = jnp.transpose(down.reshape(rows_dn, group, nb, DB), (1, 0, 2, 3)).reshape(group, -1)
    wbuf = jnp.concatenate([gu_l, dn_l], axis=1)
    wbuf = jnp.broadcast_to(wbuf[None], (zcount,) + wbuf.shape).reshape(count, -1)
    wrecv = exchange(wbuf)
    w_gu = wrecv[:, :size_gu].reshape(count * rows_gu, 2, nb, fb)
    w_dn = wrecv[:, size_gu:].reshape(count * rows_dn, nb, DB)

    def to_group(field):
        x = field.reshape(tokens, group, nb, DB)
        x = jnp.transpose(x, (1, 0, 2, 3))
        return exchange(x, "loc").reshape(group * tokens, nb, DB)

    def from_group(x):
        x = exchange(x.reshape(group, tokens, nb, DB), "loc")
        return jnp.transpose(x, (1, 0, 2, 3)).reshape(tokens, width)

    grad_out = cotangent[0]
    cot_blk = to_group(grad_out)

    xb = seq_in.reshape(nblocks, BLK, width)
    xb_peer = from_partner(xb, SEQ, top_bit)
    mixed = jnp.einsum("ij,kjd->kid", block_mix, xb, precision=HIGH).reshape(tokens, width)
    mixed_peer = jnp.einsum("ij,kjd->kid", block_mix, xb_peer, precision=HIGH).reshape(tokens, width)
    own_hi = twist_hi[side_of(top_bit)]
    first = own_hi[0] * mixed + own_hi[1] * mixed_peer
    second, first_peer = forward_section(first, twist_lo, 0)
    resid = seq_in + second
    scale = lax.rsqrt(jnp.mean(resid * resid, axis=-1, keepdims=True) + EPS)
    unit = resid * scale
    normed = unit * gain
    x_blk = to_group(normed)

    gate_val = jnp.einsum("tnd,dnf->tnf", x_blk, w_gu[:, 0], precision=HIGH)
    up_val = jnp.einsum("tnd,dnf->tnf", x_blk, w_gu[:, 1], precision=HIGH)
    sig = jax.nn.sigmoid(gate_val)
    act = gate_val * sig
    hidden = act * up_val
    grad_hidden = jnp.einsum("tnd,fnd->tnf", cot_blk, w_dn, precision=HIGH)
    grad_gate = grad_hidden * up_val * sig * (1.0 + gate_val * (1.0 - sig))
    grad_up = grad_hidden * act
    grad_x = jnp.einsum("tnf,dnf->tnd", grad_gate, w_gu[:, 0], precision=HIGH) + jnp.einsum(
        "tnf,dnf->tnd", grad_up, w_gu[:, 1], precision=HIGH
    )
    grad_normed = from_group(grad_x)

    d_gate = jnp.einsum("tnd,tnf->dnf", x_blk, grad_gate, precision=HIGH)
    d_up = jnp.einsum("tnd,tnf->dnf", x_blk, grad_up, precision=HIGH)
    d_gu = jnp.stack([d_gate, d_up], axis=1).reshape(count, -1)
    d_dn = jnp.einsum("tnf,tnd->fnd", hidden, cot_blk, precision=HIGH).reshape(count, -1)
    grecv = exchange(jnp.concatenate([d_gu, d_dn], axis=1))
    grecv = grecv.reshape(zcount, group, -1).sum(axis=0)
    part_gu = jnp.transpose(grecv[:, :size_gu].reshape(group, rows_gu, 2, nb, fb), (1, 2, 0, 3, 4))
    part_gu = part_gu.reshape(rows_gu, 2, NB, fb)
    part_down = jnp.transpose(grecv[:, size_gu:].reshape(group, rows_dn, nb, DB), (1, 0, 2, 3))
    part_down = part_down.reshape(rows_dn, NB, DB)
    n_gu = part_gu.size
    wsum = psum_doubling(jnp.concatenate([part_gu.reshape(-1), part_down.reshape(-1)]), "dp")
    part_gu = wsum[:n_gu].reshape(part_gu.shape)
    part_down = wsum[n_gu:].reshape(part_down.shape)

    grad_gain_local = jnp.sum(grad_normed * unit, axis=0)
    weighted = grad_normed * gain
    inner = jnp.mean(weighted * resid, axis=-1, keepdims=True)
    grad_resid = grad_out + scale * weighted - resid * scale * scale * scale * inner
    grad_first, term_lo = backward_section(grad_resid, first, first_peer, twist_lo, 0)
    grad_mixed, term_hi = backward_section(grad_first, mixed, mixed_peer, twist_hi, top_bit)
    grad_mb = grad_mixed.reshape(nblocks, BLK, width)
    keep = (own_hi[0] * grad_first).reshape(nblocks, BLK, width)
    give = (own_hi[1] * grad_first).reshape(nblocks, BLK, width)
    term_block = jnp.einsum("kid,kjd->ij", keep, xb, precision=HIGH) + jnp.einsum(
        "kid,kjd->ij", give, xb_peer, precision=HIGH
    )
    grad_seq = jnp.einsum("ij,kid->kjd", block_mix, grad_mb, precision=HIGH).reshape(tokens, width)
    grad_seq = grad_seq + grad_resid
    smalls = (term_block, term_hi, term_lo, grad_gain_local)
    sbuf = jnp.concatenate([t.reshape(-1) for t in smalls])
    spart = exchange(sbuf.reshape(count, -1)).sum(axis=0)
    spart = psum_doubling(spart, "dp")
    sfull = exchange(jnp.broadcast_to(spart[None], (count, spart.shape[0]))).reshape(-1)
    sums = []
    at = 0
    for t in smalls:
        sums.append(sfull[at : at + t.size].reshape(t.shape))
        at += t.size
    sum_block, sum_hi, sum_lo, sum_gain = sums
    factor = 1.0 / math.sqrt(lax.axis_size("dp") * count * tokens)
    return (
        grad_seq[None],
        part_gu * factor,
        part_down * factor,
        sum_block * factor,
        sum_hi * factor,
        sum_lo * factor,
        sum_gain * factor,
    )


def solution(mesh):
    dp_size, seq_size = mesh.devices.shape
    group = min(seq_size, NB // 2)
    split = Mesh(mesh.devices.reshape(dp_size, seq_size // group, group), ("dp",) + SEQ)
    return jax.shard_map(
        per_device,
        mesh=split,
        in_specs=(
            P("dp", SEQ, None),
            P("dp", SEQ, None),
            P(),
            P(),
            P(),
            P(),
            P(SEQ, None, None, None),
            P(SEQ, None, None),
        ),
        out_specs=(
            P("dp", SEQ, None),
            P(SEQ, None, None, None),
            P(SEQ, None, None),
            P(),
            P(),
            P(),
            P(),
        ),
        check_vma=False,
    )
```

```python
import math

import jax
import jax.numpy as jnp
from jax import lax
from jax.sharding import Mesh, PartitionSpec as P

NB = 16
BLK = 128
DB = 128


HIGH = lax.Precision.HIGHEST
EPS = 1e-05


def axis_count(axis):
    if isinstance(axis, tuple):
        return math.prod(lax.axis_size(a) for a in axis)
    return lax.axis_size(axis)


def from_partner(block, axis, distance):
    count = axis_count(axis)
    route = []
    for low in range(count):
        high = low | 1 << distance
        if high != low and high < count:
            route += [(low, high), (high, low)]
    return lax.ppermute(block, axis, route)


SEQ = ("zh", "loc")


def side_of(bit):
    return lax.axis_index(SEQ) // (1 << bit) % 2


def forward_section(field, coeff, bit):
    partner = from_partner(field, SEQ, bit)
    own = coeff[side_of(bit)]
    return (own[0] * field + own[1] * partner, partner)


def backward_section(grad, field, partner, coeff, bit):
    side = side_of(bit)
    own = coeff[side]
    sent = from_partner(own[1] * grad, SEQ, bit)
    back = own[0] * grad + sent
    term = jnp.stack([jnp.sum(grad * field, axis=0), jnp.sum(grad * partner, axis=0)])
    pick = (jnp.arange(2) == side).astype(jnp.float32)
    return (back, pick[:, None, None] * term[None])


def psum_doubling(x, axis):
    for bit in range(axis_count(axis).bit_length() - 1):
        x = x + from_partner(x, axis, bit)
    return x


def exchange(x, axis=SEQ):
    return lax.all_to_all(x, axis, 0, 0, tiled=True)


def per_device(inputs, cotangent, block_mix, twist_hi, twist_lo, gain, gate_up, down):
    seq_in = inputs[0]
    tokens, width = seq_in.shape
    count = axis_count(SEQ)
    group = lax.axis_size("loc")
    zcount = count // group
    nb = NB // group
    top_bit = count.bit_length() - 2
    nblocks = tokens // BLK
    rows_gu = gate_up.shape[0]
    rows_dn = down.shape[0]
    fb = gate_up.shape[3]
    size_gu = rows_gu * 2 * nb * fb

    gu_l = jnp.transpose(gate_up.reshape(rows_gu, 2, group, nb, fb), (2, 0, 1, 3, 4)).reshape(group, -1)
    dn_l = jnp.transpose(down.reshape(rows_dn, group, nb, DB), (1, 0, 2, 3)).reshape(group, -1)
    wbuf = jnp.concatenate([gu_l, dn_l], axis=1)
    wbuf = jnp.broadcast_to(wbuf[None], (zcount,) + wbuf.shape).reshape(count, -1)
    wrecv = exchange(wbuf)
    w_gu = wrecv[:, :size_gu].reshape(count * rows_gu, 2, nb, fb)
    w_dn = wrecv[:, size_gu:].reshape(count * rows_dn, nb, DB)

    def to_group(field):
        x = field.reshape(tokens, group, nb, DB)
        x = jnp.transpose(x, (1, 0, 2, 3))
        return exchange(x, "loc").reshape(group * tokens, nb, DB)

    def from_group(x):
        x = exchange(x.reshape(group, tokens, nb, DB), "loc")
        return jnp.transpose(x, (1, 0, 2, 3)).reshape(tokens, width)

    grad_out = cotangent[0]
    cot_blk = to_group(grad_out)

    xb = seq_in.reshape(nblocks, BLK, width)
    xb_peer = from_partner(xb, SEQ, top_bit)
    mixed = jnp.einsum("ij,kjd->kid", block_mix, xb, precision=HIGH).reshape(tokens, width)
    mixed_peer = jnp.einsum("ij,kjd->kid", block_mix, xb_peer, precision=HIGH).reshape(tokens, width)
    own_hi = twist_hi[side_of(top_bit)]
    first = own_hi[0] * mixed + own_hi[1] * mixed_peer
    second, first_peer = forward_section(first, twist_lo, 0)
    resid = seq_in + second
    scale = lax.rsqrt(jnp.mean(resid * resid, axis=-1, keepdims=True) + EPS)
    unit = resid * scale
    normed = unit * gain
    x_blk = to_group(normed)

    gate_val = jnp.einsum("tnd,dnf->tnf", x_blk, w_gu[:, 0], precision=HIGH)
    up_val = jnp.einsum("tnd,dnf->tnf", x_blk, w_gu[:, 1], precision=HIGH)
    sig = jax.nn.sigmoid(gate_val)
    act = gate_val * sig
    hidden = act * up_val
    grad_hidden = jnp.einsum("tnd,fnd->tnf", cot_blk, w_dn, precision=HIGH)
    grad_gate = grad_hidden * up_val * sig * (1.0 + gate_val * (1.0 - sig))
    grad_up = grad_hidden * act
    grad_x = jnp.einsum("tnf,dnf->tnd", grad_gate, w_gu[:, 0], precision=HIGH) + jnp.einsum(
        "tnf,dnf->tnd", grad_up, w_gu[:, 1], precision=HIGH
    )
    grad_normed = from_group(grad_x)

    d_gate = jnp.einsum("tnd,tnf->dnf", x_blk, grad_gate, precision=HIGH)
    d_up = jnp.einsum("tnd,tnf->dnf", x_blk, grad_up, precision=HIGH)
    d_gu = jnp.stack([d_gate, d_up], axis=1).reshape(count, -1)
    d_dn = jnp.einsum("tnf,tnd->fnd", hidden, cot_blk, precision=HIGH).reshape(count, -1)
    grecv = exchange(jnp.concatenate([d_gu, d_dn], axis=1))
    grecv = grecv.reshape(zcount, group, -1).sum(axis=0)
    part_gu = jnp.transpose(grecv[:, :size_gu].reshape(group, rows_gu, 2, nb, fb), (1, 2, 0, 3, 4))
    part_gu = part_gu.reshape(rows_gu, 2, NB, fb)
    part_down = jnp.transpose(grecv[:, size_gu:].reshape(group, rows_dn, nb, DB), (1, 0, 2, 3))
    part_down = part_down.reshape(rows_dn, NB, DB)
    n_gu = part_gu.size
    wsum = psum_doubling(jnp.concatenate([part_gu.reshape(-1), part_down.reshape(-1)]), "dp")
    part_gu = wsum[:n_gu].reshape(part_gu.shape)
    part_down = wsum[n_gu:].reshape(part_down.shape)

    grad_gain_local = jnp.sum(grad_normed * unit, axis=0)
    weighted = grad_normed * gain
    inner = jnp.mean(weighted * resid, axis=-1, keepdims=True)
    grad_resid = grad_out + scale * weighted - resid * scale * scale * scale * inner
    far_back = own_hi[0] * grad_resid + from_partner(own_hi[1] * grad_resid, SEQ, top_bit)
    grad_first, term_lo = backward_section(grad_resid, first, first_peer, twist_lo, 0)
    _, term_hi = backward_section(grad_first, mixed, mixed_peer, twist_hi, top_bit)
    own_lo = twist_lo[side_of(0)]
    grad_mixed = own_lo[0] * far_back + from_partner(own_lo[1] * far_back, SEQ, 0)
    grad_mb = grad_mixed.reshape(nblocks, BLK, width)
    keep = (own_hi[0] * grad_first).reshape(nblocks, BLK, width)
    give = (own_hi[1] * grad_first).reshape(nblocks, BLK, width)
    term_block = jnp.einsum("kid,kjd->ij", keep, xb, precision=HIGH) + jnp.einsum(
        "kid,kjd->ij", give, xb_peer, precision=HIGH
    )
    grad_seq = jnp.einsum("ij,kid->kjd", block_mix, grad_mb, precision=HIGH).reshape(tokens, width)
    grad_seq = grad_seq + grad_resid
    smalls = (term_block, term_hi, term_lo, grad_gain_local)
    sbuf = jnp.concatenate([t.reshape(-1) for t in smalls])
    spart = exchange(sbuf.reshape(count, -1)).sum(axis=0)
    spart = psum_doubling(spart, "dp")
    sfull = exchange(jnp.broadcast_to(spart[None], (count, spart.shape[0]))).reshape(-1)
    sums = []
    at = 0
    for t in smalls:
        sums.append(sfull[at : at + t.size].reshape(t.shape))
        at += t.size
    sum_block, sum_hi, sum_lo, sum_gain = sums
    factor = 1.0 / math.sqrt(lax.axis_size("dp") * count * tokens)
    return (
        grad_seq[None],
        part_gu * factor,
        part_down * factor,
        sum_block * factor,
        sum_hi * factor,
        sum_lo * factor,
        sum_gain * factor,
    )


def solution(mesh):
    dp_size, seq_size = mesh.devices.shape
    group = min(seq_size, NB // 2)
    split = Mesh(mesh.devices.reshape(dp_size, seq_size // group, group), ("dp",) + SEQ)
    return jax.shard_map(
        per_device,
        mesh=split,
        in_specs=(
            P("dp", SEQ, None),
            P("dp", SEQ, None),
            P(),
            P(),
            P(),
            P(),
            P(SEQ, None, None, None),
            P(SEQ, None, None),
        ),
        out_specs=(
            P("dp", SEQ, None),
            P(SEQ, None, None, None),
            P(SEQ, None, None),
            P(),
            P(),
            P(),
            P(),
        ),
        check_vma=False,
    )
```

```python
import math

import jax
import jax.numpy as jnp
from jax import lax
from jax.sharding import Mesh, PartitionSpec as P

NB = 16
BLK = 128
DB = 128


HIGH = lax.Precision.HIGHEST
EPS = 1e-05


def axis_count(axis):
    if isinstance(axis, tuple):
        return math.prod(lax.axis_size(a) for a in axis)
    return lax.axis_size(axis)


def from_partner(block, axis, distance):
    count = axis_count(axis)
    route = []
    for low in range(count):
        high = low | 1 << distance
        if high != low and high < count:
            route += [(low, high), (high, low)]
    return lax.ppermute(block, axis, route)


SEQ = ("zh", "loc")


def side_of(bit):
    return lax.axis_index(SEQ) // (1 << bit) % 2


def forward_section(field, coeff, bit):
    partner = from_partner(field, SEQ, bit)
    own = coeff[side_of(bit)]
    return (own[0] * field + own[1] * partner, partner)


def backward_section(grad, field, partner, coeff, bit):
    side = side_of(bit)
    own = coeff[side]
    sent = from_partner(own[1] * grad, SEQ, bit)
    back = own[0] * grad + sent
    term = jnp.stack([jnp.sum(grad * field, axis=0), jnp.sum(grad * partner, axis=0)])
    pick = (jnp.arange(2) == side).astype(jnp.float32)
    return (back, pick[:, None, None] * term[None])


def psum_doubling(x, axis):
    for bit in range(axis_count(axis).bit_length() - 1):
        x = x + from_partner(x, axis, bit)
    return x


def exchange(x, axis=SEQ):
    return lax.all_to_all(x, axis, 0, 0, tiled=True)


def per_device(inputs, cotangent, block_mix, twist_hi, twist_lo, gain, gate_up, down):
    seq_in = inputs[0]
    tokens, width = seq_in.shape
    count = axis_count(SEQ)
    group = lax.axis_size("loc")
    zcount = count // group
    nb = NB // group
    top_bit = count.bit_length() - 2
    nblocks = tokens // BLK
    rows_gu = gate_up.shape[0]
    rows_dn = down.shape[0]
    fb = gate_up.shape[3]
    size_gu = rows_gu * 2 * nb * fb

    gu_l = jnp.transpose(gate_up.reshape(rows_gu, 2, group, nb, fb), (2, 0, 1, 3, 4)).reshape(group, -1)
    dn_l = jnp.transpose(down.reshape(rows_dn, group, nb, DB), (1, 0, 2, 3)).reshape(group, -1)
    wbuf = jnp.concatenate([gu_l, dn_l], axis=1)
    wbuf = jnp.broadcast_to(wbuf[None], (zcount,) + wbuf.shape).reshape(count, -1)
    wrecv = exchange(wbuf)
    w_gu = wrecv[:, :size_gu].reshape(count * rows_gu, 2, nb, fb)
    w_dn = wrecv[:, size_gu:].reshape(count * rows_dn, nb, DB)

    def to_group(field):
        x = field.reshape(tokens, group, nb, DB)
        x = jnp.transpose(x, (1, 0, 2, 3))
        return exchange(x, "loc").reshape(group * tokens, nb, DB)

    def from_group(x):
        x = exchange(x.reshape(group, tokens, nb, DB), "loc")
        return jnp.transpose(x, (1, 0, 2, 3)).reshape(tokens, width)

    grad_out = cotangent[0]
    cot_blk = to_group(grad_out)

    xb = seq_in.reshape(nblocks, BLK, width)
    xb_peer = from_partner(xb, SEQ, top_bit)
    mixed = jnp.einsum("ij,kjd->kid", block_mix, xb, precision=HIGH).reshape(tokens, width)
    mixed_peer = jnp.einsum("ij,kjd->kid", block_mix, xb_peer, precision=HIGH).reshape(tokens, width)
    own_hi = twist_hi[side_of(top_bit)]
    first = own_hi[0] * mixed + own_hi[1] * mixed_peer
    second, first_peer = forward_section(first, twist_lo, 0)
    resid = seq_in + second
    scale = lax.rsqrt(jnp.mean(resid * resid, axis=-1, keepdims=True) + EPS)
    unit = resid * scale
    normed = unit * gain
    x_blk = to_group(normed)

    gate_val = jnp.einsum("tnd,dnf->tnf", x_blk, w_gu[:, 0], precision=HIGH)
    up_val = jnp.einsum("tnd,dnf->tnf", x_blk, w_gu[:, 1], precision=HIGH)
    sig = jax.nn.sigmoid(gate_val)
    act = gate_val * sig
    hidden = act * up_val
    grad_hidden = jnp.einsum("tnd,fnd->tnf", cot_blk, w_dn, precision=HIGH)
    grad_gate = grad_hidden * up_val * sig * (1.0 + gate_val * (1.0 - sig))
    grad_up = grad_hidden * act
    grad_x = jnp.einsum("tnf,dnf->tnd", grad_gate, w_gu[:, 0], precision=HIGH) + jnp.einsum(
        "tnf,dnf->tnd", grad_up, w_gu[:, 1], precision=HIGH
    )
    grad_normed = from_group(grad_x)

    d_gate = jnp.einsum("tnd,tnf->dnf", x_blk, grad_gate, precision=HIGH)
    d_up = jnp.einsum("tnd,tnf->dnf", x_blk, grad_up, precision=HIGH)
    d_gu = jnp.stack([d_gate, d_up], axis=1).reshape(count, -1)
    d_dn = jnp.einsum("tnf,tnd->fnd", hidden, cot_blk, precision=HIGH).reshape(count, -1)
    grecv = exchange(jnp.concatenate([d_gu, d_dn], axis=1))
    grecv = grecv.reshape(zcount, group, -1).sum(axis=0)
    part_gu = jnp.transpose(grecv[:, :size_gu].reshape(group, rows_gu, 2, nb, fb), (1, 2, 0, 3, 4))
    part_gu = part_gu.reshape(rows_gu, 2, NB, fb)
    part_down = jnp.transpose(grecv[:, size_gu:].reshape(group, rows_dn, nb, DB), (1, 0, 2, 3))
    part_down = part_down.reshape(rows_dn, NB, DB)
    n_gu = part_gu.size
    wsum = psum_doubling(jnp.concatenate([part_gu.reshape(-1), part_down.reshape(-1)]), "dp")

    grad_gain_local = jnp.sum(grad_normed * unit, axis=0)
    weighted = grad_normed * gain
    inner = jnp.mean(weighted * resid, axis=-1, keepdims=True)
    grad_resid = grad_out + scale * weighted - resid * scale * scale * scale * inner
    far_send, wsum = lax.optimization_barrier((own_hi[1] * grad_resid, wsum))
    far_recv = from_partner(far_send, SEQ, top_bit)
    far_back = own_hi[0] * grad_resid + far_recv
    grad_first, term_lo = backward_section(grad_resid, first, first_peer, twist_lo, 0)
    _, term_hi = backward_section(grad_first, mixed, mixed_peer, twist_hi, top_bit)
    own_lo = twist_lo[side_of(0)]
    grad_mixed = own_lo[0] * far_back + from_partner(own_lo[1] * far_back, SEQ, 0)
    grad_mb = grad_mixed.reshape(nblocks, BLK, width)
    keep = (own_hi[0] * grad_first).reshape(nblocks, BLK, width)
    give = (own_hi[1] * grad_first).reshape(nblocks, BLK, width)
    term_block = jnp.einsum("kid,kjd->ij", keep, xb, precision=HIGH) + jnp.einsum(
        "kid,kjd->ij", give, xb_peer, precision=HIGH
    )
    grad_seq = jnp.einsum("ij,kid->kjd", block_mix, grad_mb, precision=HIGH).reshape(tokens, width)
    grad_seq = grad_seq + grad_resid
    smalls = (term_block, term_hi, term_lo, grad_gain_local)
    sbuf = jnp.concatenate([t.reshape(-1) for t in smalls])
    z_bits = [("dp", 0)] + [(SEQ, b) for b in range(group.bit_length() - 1, count.bit_length() - 1)]
    off_z = [(SEQ, b) for b in range(group.bit_length() - 1)]
    off_z += [("dp", b) for b in range(1, lax.axis_size("dp").bit_length() - 1)]
    sfull = sbuf
    for axis, bit in off_z:
        sfull = sfull + from_partner(sfull, axis, bit)
    sfull, far_recv = lax.optimization_barrier((sfull, far_recv))
    for axis, bit in z_bits:
        sfull = sfull + from_partner(sfull, axis, bit)
    sums = []
    at = 0
    for t in smalls:
        sums.append(sfull[at : at + t.size].reshape(t.shape))
        at += t.size
    sum_block, sum_hi, sum_lo, sum_gain = sums
    factor = 1.0 / math.sqrt(lax.axis_size("dp") * count * tokens)
    part_gu = wsum[:n_gu].reshape(part_gu.shape)
    part_down = wsum[n_gu:].reshape(part_down.shape)
    return (
        grad_seq[None],
        part_gu * factor,
        part_down * factor,
        sum_block * factor,
        sum_hi * factor,
        sum_lo * factor,
        sum_gain * factor,
    )


def solution(mesh):
    dp_size, seq_size = mesh.devices.shape
    group = min(seq_size, NB // 2)
    split = Mesh(mesh.devices.reshape(dp_size, seq_size // group, group), ("dp",) + SEQ)
    return jax.shard_map(
        per_device,
        mesh=split,
        in_specs=(
            P("dp", SEQ, None),
            P("dp", SEQ, None),
            P(),
            P(),
            P(),
            P(),
            P(SEQ, None, None, None),
            P(SEQ, None, None),
        ),
        out_specs=(
            P("dp", SEQ, None),
            P(SEQ, None, None, None),
            P(SEQ, None, None),
            P(),
            P(),
            P(),
            P(),
        ),
        check_vma=False,
    )
```

```python
import math

import jax
import jax.numpy as jnp
from jax import lax
from jax.sharding import Mesh, PartitionSpec as P

NB = 16
BLK = 128
DB = 128


HIGH = lax.Precision.HIGHEST
EPS = 1e-05


def axis_count(axis):
    if isinstance(axis, tuple):
        return math.prod(lax.axis_size(a) for a in axis)
    return lax.axis_size(axis)


def from_partner(block, axis, distance):
    count = axis_count(axis)
    route = []
    for low in range(count):
        high = low | 1 << distance
        if high != low and high < count:
            route += [(low, high), (high, low)]
    return lax.ppermute(block, axis, route)


SEQ = ("zh", "loc")


def side_of(bit):
    return lax.axis_index(SEQ) // (1 << bit) % 2


def forward_section(field, coeff, bit):
    partner = from_partner(field, SEQ, bit)
    own = coeff[side_of(bit)]
    return (own[0] * field + own[1] * partner, partner)


def backward_section(grad, field, partner, coeff, bit):
    side = side_of(bit)
    own = coeff[side]
    sent = from_partner(own[1] * grad, SEQ, bit)
    back = own[0] * grad + sent
    term = jnp.stack([jnp.sum(grad * field, axis=0), jnp.sum(grad * partner, axis=0)])
    pick = (jnp.arange(2) == side).astype(jnp.float32)
    return (back, pick[:, None, None] * term[None])


def psum_doubling(x, axis):
    for bit in range(axis_count(axis).bit_length() - 1):
        x = x + from_partner(x, axis, bit)
    return x


def exchange(x, axis=SEQ):
    return lax.all_to_all(x, axis, 0, 0, tiled=True)


def per_device(inputs, cotangent, block_mix, twist_hi, twist_lo, gain, gate_up, down):
    seq_in = inputs[0]
    tokens, width = seq_in.shape
    count = axis_count(SEQ)
    group = lax.axis_size("loc")
    zcount = count // group
    nb = NB // group
    top_bit = count.bit_length() - 2
    nblocks = tokens // BLK
    rows_gu = gate_up.shape[0]
    rows_dn = down.shape[0]
    fb = gate_up.shape[3]
    size_gu = rows_gu * 2 * nb * fb

    gu_l = jnp.transpose(gate_up.reshape(rows_gu, 2, group, nb, fb), (2, 0, 1, 3, 4)).reshape(group, -1)
    dn_l = jnp.transpose(down.reshape(rows_dn, group, nb, DB), (1, 0, 2, 3)).reshape(group, -1)
    wbuf = jnp.concatenate([gu_l, dn_l], axis=1)
    wbuf = jnp.broadcast_to(wbuf[None], (zcount,) + wbuf.shape).reshape(count, -1)
    wrecv = exchange(wbuf)
    w_gu = wrecv[:, :size_gu].reshape(count * rows_gu, 2, nb, fb)
    w_dn = wrecv[:, size_gu:].reshape(count * rows_dn, nb, DB)

    def to_group(field):
        x = field.reshape(tokens, group, nb, DB)
        x = jnp.transpose(x, (1, 0, 2, 3))
        return exchange(x, "loc").reshape(group * tokens, nb, DB)

    def from_group(x):
        x = exchange(x.reshape(group, tokens, nb, DB), "loc")
        return jnp.transpose(x, (1, 0, 2, 3)).reshape(tokens, width)

    grad_out = cotangent[0]
    cot_blk = to_group(grad_out)

    xb = seq_in.reshape(nblocks, BLK, width)
    xb_peer = from_partner(xb, SEQ, top_bit)
    mixed = jnp.einsum("ij,kjd->kid", block_mix, xb, precision=HIGH).reshape(tokens, width)
    mixed_peer = jnp.einsum("ij,kjd->kid", block_mix, xb_peer, precision=HIGH).reshape(tokens, width)
    own_hi = twist_hi[side_of(top_bit)]
    first = own_hi[0] * mixed + own_hi[1] * mixed_peer
    second, first_peer = forward_section(first, twist_lo, 0)
    resid = seq_in + second
    scale = lax.rsqrt(jnp.mean(resid * resid, axis=-1, keepdims=True) + EPS)
    unit = resid * scale
    normed = unit * gain
    x_blk = to_group(normed)

    gate_val = jnp.einsum("tnd,dnf->tnf", x_blk, w_gu[:, 0], precision=HIGH)
    up_val = jnp.einsum("tnd,dnf->tnf", x_blk, w_gu[:, 1], precision=HIGH)
    sig = jax.nn.sigmoid(gate_val)
    act = gate_val * sig
    hidden = act * up_val
    grad_hidden = jnp.einsum("tnd,fnd->tnf", cot_blk, w_dn, precision=HIGH)
    grad_gate = grad_hidden * up_val * sig * (1.0 + gate_val * (1.0 - sig))
    grad_up = grad_hidden * act
    grad_x = jnp.einsum("tnf,dnf->tnd", grad_gate, w_gu[:, 0], precision=HIGH) + jnp.einsum(
        "tnf,dnf->tnd", grad_up, w_gu[:, 1], precision=HIGH
    )
    grad_normed = from_group(grad_x)

    d_gate = jnp.einsum("tnd,tnf->dnf", x_blk, grad_gate, precision=HIGH)
    d_up = jnp.einsum("tnd,tnf->dnf", x_blk, grad_up, precision=HIGH)
    d_gu = jnp.stack([d_gate, d_up], axis=1).reshape(count, -1)
    d_dn = jnp.einsum("tnf,tnd->fnd", hidden, cot_blk, precision=HIGH).reshape(count, -1)
    wsend = jnp.concatenate([d_gu, d_dn], axis=1)

    grad_gain_local = jnp.sum(grad_normed * unit, axis=0)
    weighted = grad_normed * gain
    inner = jnp.mean(weighted * resid, axis=-1, keepdims=True)
    grad_resid = grad_out + scale * weighted - resid * scale * scale * scale * inner
    far_recv = from_partner(own_hi[1] * grad_resid, SEQ, top_bit)
    far_back = own_hi[0] * grad_resid + far_recv
    wsend, _ = lax.optimization_barrier((wsend, far_recv))
    grecv = exchange(wsend)
    grecv = grecv.reshape(zcount, group, -1).sum(axis=0)
    part_gu = jnp.transpose(grecv[:, :size_gu].reshape(group, rows_gu, 2, nb, fb), (1, 2, 0, 3, 4))
    part_gu = part_gu.reshape(rows_gu, 2, NB, fb)
    part_down = jnp.transpose(grecv[:, size_gu:].reshape(group, rows_dn, nb, DB), (1, 0, 2, 3))
    part_down = part_down.reshape(rows_dn, NB, DB)
    n_gu = part_gu.size
    wsum = psum_doubling(jnp.concatenate([part_gu.reshape(-1), part_down.reshape(-1)]), "dp")
    grad_first, term_lo = backward_section(grad_resid, first, first_peer, twist_lo, 0)
    _, term_hi = backward_section(grad_first, mixed, mixed_peer, twist_hi, top_bit)
    own_lo = twist_lo[side_of(0)]
    grad_mixed = own_lo[0] * far_back + from_partner(own_lo[1] * far_back, SEQ, 0)
    grad_mb = grad_mixed.reshape(nblocks, BLK, width)
    keep = (own_hi[0] * grad_first).reshape(nblocks, BLK, width)
    give = (own_hi[1] * grad_first).reshape(nblocks, BLK, width)
    term_block = jnp.einsum("kid,kjd->ij", keep, xb, precision=HIGH) + jnp.einsum(
        "kid,kjd->ij", give, xb_peer, precision=HIGH
    )
    grad_seq = jnp.einsum("ij,kid->kjd", block_mix, grad_mb, precision=HIGH).reshape(tokens, width)
    grad_seq = grad_seq + grad_resid
    smalls = (term_block, term_hi, term_lo, grad_gain_local)
    sbuf = jnp.concatenate([t.reshape(-1) for t in smalls])
    z_bits = [("dp", 0)] + [(SEQ, b) for b in range(group.bit_length() - 1, count.bit_length() - 1)]
    off_z = [(SEQ, b) for b in range(group.bit_length() - 1)]
    off_z += [("dp", b) for b in range(1, lax.axis_size("dp").bit_length() - 1)]
    sfull = sbuf
    for axis, bit in off_z:
        sfull = sfull + from_partner(sfull, axis, bit)
    sfull, far_recv = lax.optimization_barrier((sfull, far_recv))
    for axis, bit in z_bits:
        sfull = sfull + from_partner(sfull, axis, bit)
    sums = []
    at = 0
    for t in smalls:
        sums.append(sfull[at : at + t.size].reshape(t.shape))
        at += t.size
    sum_block, sum_hi, sum_lo, sum_gain = sums
    factor = 1.0 / math.sqrt(lax.axis_size("dp") * count * tokens)
    part_gu = wsum[:n_gu].reshape(part_gu.shape)
    part_down = wsum[n_gu:].reshape(part_down.shape)
    return (
        grad_seq[None],
        part_gu * factor,
        part_down * factor,
        sum_block * factor,
        sum_hi * factor,
        sum_lo * factor,
        sum_gain * factor,
    )


def solution(mesh):
    dp_size, seq_size = mesh.devices.shape
    group = min(seq_size, NB // 2)
    split = Mesh(mesh.devices.reshape(dp_size, seq_size // group, group), ("dp",) + SEQ)
    return jax.shard_map(
        per_device,
        mesh=split,
        in_specs=(
            P("dp", SEQ, None),
            P("dp", SEQ, None),
            P(),
            P(),
            P(),
            P(),
            P(SEQ, None, None, None),
            P(SEQ, None, None),
        ),
        out_specs=(
            P("dp", SEQ, None),
            P(SEQ, None, None, None),
            P(SEQ, None, None),
            P(),
            P(),
            P(),
            P(),
        ),
        check_vma=False,
    )
```

```python
import math

import jax
import jax.numpy as jnp
from jax import lax
from jax.sharding import Mesh, PartitionSpec as P

NB = 16
BLK = 128
DB = 128


HIGH = lax.Precision.HIGHEST
EPS = 1e-05


def axis_count(axis):
    if isinstance(axis, tuple):
        return math.prod(lax.axis_size(a) for a in axis)
    return lax.axis_size(axis)


def from_partner(block, axis, distance):
    count = axis_count(axis)
    route = []
    for low in range(count):
        high = low | 1 << distance
        if high != low and high < count:
            route += [(low, high), (high, low)]
    return lax.ppermute(block, axis, route)


SEQ = ("zh", "loc")


def side_of(bit):
    return lax.axis_index(SEQ) // (1 << bit) % 2


def forward_section(field, coeff, bit):
    partner = from_partner(field, SEQ, bit)
    own = coeff[side_of(bit)]
    return (own[0] * field + own[1] * partner, partner)


def backward_section(grad, field, partner, coeff, bit):
    side = side_of(bit)
    own = coeff[side]
    sent = from_partner(own[1] * grad, SEQ, bit)
    back = own[0] * grad + sent
    term = jnp.stack([jnp.sum(grad * field, axis=0), jnp.sum(grad * partner, axis=0)])
    pick = (jnp.arange(2) == side).astype(jnp.float32)
    return (back, pick[:, None, None] * term[None])


def psum_doubling(x, axis):
    for bit in range(axis_count(axis).bit_length() - 1):
        x = x + from_partner(x, axis, bit)
    return x


def exchange(x, axis=SEQ):
    return lax.all_to_all(x, axis, 0, 0, tiled=True)


def per_device(inputs, cotangent, block_mix, twist_hi, twist_lo, gain, gate_up, down):
    seq_in = inputs[0]
    tokens, width = seq_in.shape
    count = axis_count(SEQ)
    group = lax.axis_size("loc")
    zcount = count // group
    nb = NB // group
    top_bit = count.bit_length() - 2
    nblocks = tokens // BLK
    rows_gu = gate_up.shape[0]
    rows_dn = down.shape[0]
    fb = gate_up.shape[3]
    size_gu = rows_gu * 2 * nb * fb

    gu_l = jnp.transpose(gate_up.reshape(rows_gu, 2, group, nb, fb), (2, 0, 1, 3, 4)).reshape(group, -1)
    dn_l = jnp.transpose(down.reshape(rows_dn, group, nb, DB), (1, 0, 2, 3)).reshape(group, -1)
    wbuf = jnp.concatenate([gu_l, dn_l], axis=1)
    wbuf = jnp.broadcast_to(wbuf[None], (zcount,) + wbuf.shape).reshape(count, -1)
    wrecv = exchange(wbuf)
    w_gu = wrecv[:, :size_gu].reshape(count * rows_gu, 2, nb, fb)
    w_dn = wrecv[:, size_gu:].reshape(count * rows_dn, nb, DB)

    def to_group(field):
        x = field.reshape(tokens, group, nb, -1)
        x = jnp.transpose(x, (1, 0, 2, 3))
        return exchange(x, "loc").reshape(group * tokens, nb, -1)

    def from_group(x):
        x = exchange(x.reshape(group, tokens, nb, DB), "loc")
        return jnp.transpose(x, (1, 0, 2, 3)).reshape(tokens, width)

    grad_out = cotangent[0]

    xb = seq_in.reshape(nblocks, BLK, width)
    xb_peer = from_partner(xb, SEQ, top_bit)
    mixed = jnp.einsum("ij,kjd->kid", block_mix, xb, precision=HIGH).reshape(tokens, width)
    mixed_peer = jnp.einsum("ij,kjd->kid", block_mix, xb_peer, precision=HIGH).reshape(tokens, width)
    own_hi = twist_hi[side_of(top_bit)]
    first = own_hi[0] * mixed + own_hi[1] * mixed_peer
    second, first_peer = forward_section(first, twist_lo, 0)
    resid = seq_in + second
    scale = lax.rsqrt(jnp.mean(resid * resid, axis=-1, keepdims=True) + EPS)
    unit = resid * scale
    normed = unit * gain
    both = to_group(jnp.concatenate([normed.reshape(tokens, NB, DB), grad_out.reshape(tokens, NB, DB)], axis=2))
    x_blk = both[..., :DB]
    cot_blk = both[..., DB:]

    gate_val = jnp.einsum("tnd,dnf->tnf", x_blk, w_gu[:, 0], precision=HIGH)
    up_val = jnp.einsum("tnd,dnf->tnf", x_blk, w_gu[:, 1], precision=HIGH)
    sig = jax.nn.sigmoid(gate_val)
    act = gate_val * sig
    hidden = act * up_val
    grad_hidden = jnp.einsum("tnd,fnd->tnf", cot_blk, w_dn, precision=HIGH)
    grad_gate = grad_hidden * up_val * sig * (1.0 + gate_val * (1.0 - sig))
    grad_up = grad_hidden * act
    grad_x = jnp.einsum("tnf,dnf->tnd", grad_gate, w_gu[:, 0], precision=HIGH) + jnp.einsum(
        "tnf,dnf->tnd", grad_up, w_gu[:, 1], precision=HIGH
    )
    grad_normed = from_group(grad_x)

    d_gate = jnp.einsum("tnd,tnf->dnf", x_blk, grad_gate, precision=HIGH)
    d_up = jnp.einsum("tnd,tnf->dnf", x_blk, grad_up, precision=HIGH)
    d_gu = jnp.stack([d_gate, d_up], axis=1).reshape(count, -1)
    d_dn = jnp.einsum("tnf,tnd->fnd", hidden, cot_blk, precision=HIGH).reshape(count, -1)
    grecv = exchange(jnp.concatenate([d_gu, d_dn], axis=1))
    grecv = grecv.reshape(zcount, group, -1).sum(axis=0)
    part_gu = jnp.transpose(grecv[:, :size_gu].reshape(group, rows_gu, 2, nb, fb), (1, 2, 0, 3, 4))
    part_gu = part_gu.reshape(rows_gu, 2, NB, fb)
    part_down = jnp.transpose(grecv[:, size_gu:].reshape(group, rows_dn, nb, DB), (1, 0, 2, 3))
    part_down = part_down.reshape(rows_dn, NB, DB)
    n_gu = part_gu.size
    wsum = psum_doubling(jnp.concatenate([part_gu.reshape(-1), part_down.reshape(-1)]), "dp")
    part_gu = wsum[:n_gu].reshape(part_gu.shape)
    part_down = wsum[n_gu:].reshape(part_down.shape)

    grad_gain_local = jnp.sum(grad_normed * unit, axis=0)
    weighted = grad_normed * gain
    inner = jnp.mean(weighted * resid, axis=-1, keepdims=True)
    grad_resid = grad_out + scale * weighted - resid * scale * scale * scale * inner
    grad_first, term_lo = backward_section(grad_resid, first, first_peer, twist_lo, 0)
    grad_mixed, term_hi = backward_section(grad_first, mixed, mixed_peer, twist_hi, top_bit)
    grad_mb = grad_mixed.reshape(nblocks, BLK, width)
    keep = (own_hi[0] * grad_first).reshape(nblocks, BLK, width)
    give = (own_hi[1] * grad_first).reshape(nblocks, BLK, width)
    term_block = jnp.einsum("kid,kjd->ij", keep, xb, precision=HIGH) + jnp.einsum(
        "kid,kjd->ij", give, xb_peer, precision=HIGH
    )
    grad_seq = jnp.einsum("ij,kid->kjd", block_mix, grad_mb, precision=HIGH).reshape(tokens, width)
    grad_seq = grad_seq + grad_resid
    smalls = (term_block, term_hi, term_lo, grad_gain_local)
    sbuf = jnp.concatenate([t.reshape(-1) for t in smalls])
    spart = exchange(sbuf.reshape(count, -1)).sum(axis=0)
    spart = psum_doubling(spart, "dp")
    sfull = exchange(jnp.broadcast_to(spart[None], (count, spart.shape[0]))).reshape(-1)
    sums = []
    at = 0
    for t in smalls:
        sums.append(sfull[at : at + t.size].reshape(t.shape))
        at += t.size
    sum_block, sum_hi, sum_lo, sum_gain = sums
    factor = 1.0 / math.sqrt(lax.axis_size("dp") * count * tokens)
    return (
        grad_seq[None],
        part_gu * factor,
        part_down * factor,
        sum_block * factor,
        sum_hi * factor,
        sum_lo * factor,
        sum_gain * factor,
    )


def solution(mesh):
    dp_size, seq_size = mesh.devices.shape
    group = min(seq_size, NB // 2)
    split = Mesh(mesh.devices.reshape(dp_size, seq_size // group, group), ("dp",) + SEQ)
    return jax.shard_map(
        per_device,
        mesh=split,
        in_specs=(
            P("dp", SEQ, None),
            P("dp", SEQ, None),
            P(),
            P(),
            P(),
            P(),
            P(SEQ, None, None, None),
            P(SEQ, None, None),
        ),
        out_specs=(
            P("dp", SEQ, None),
            P(SEQ, None, None, None),
            P(SEQ, None, None),
            P(),
            P(),
            P(),
            P(),
        ),
        check_vma=False,
    )
```

```python
import math

import jax
import jax.numpy as jnp
from jax import lax
from jax.sharding import Mesh, PartitionSpec as P

NB = 16
BLK = 128
DB = 128


HIGH = lax.Precision.HIGHEST
EPS = 1e-05


def axis_count(axis):
    if isinstance(axis, tuple):
        return math.prod(lax.axis_size(a) for a in axis)
    return lax.axis_size(axis)


def from_partner(block, axis, distance):
    count = axis_count(axis)
    route = []
    for low in range(count):
        high = low | 1 << distance
        if high != low and high < count:
            route += [(low, high), (high, low)]
    return lax.ppermute(block, axis, route)


SEQ = ("zh", "loc")


def side_of(bit):
    return lax.axis_index(SEQ) // (1 << bit) % 2


def forward_section(field, coeff, bit):
    partner = from_partner(field, SEQ, bit)
    own = coeff[side_of(bit)]
    return (own[0] * field + own[1] * partner, partner)


def backward_section(grad, field, partner, coeff, bit):
    side = side_of(bit)
    own = coeff[side]
    sent = from_partner(own[1] * grad, SEQ, bit)
    back = own[0] * grad + sent
    term = jnp.stack([jnp.sum(grad * field, axis=0), jnp.sum(grad * partner, axis=0)])
    pick = (jnp.arange(2) == side).astype(jnp.float32)
    return (back, pick[:, None, None] * term[None])


def psum_doubling(x, axis):
    for bit in range(axis_count(axis).bit_length() - 1):
        x = x + from_partner(x, axis, bit)
    return x


def exchange(x, axis=SEQ):
    return lax.all_to_all(x, axis, 0, 0, tiled=True)


def per_device(inputs, cotangent, block_mix, twist_hi, twist_lo, gain, gate_up, down):
    seq_in = inputs[0]
    tokens, width = seq_in.shape
    count = axis_count(SEQ)
    group = lax.axis_size("loc")
    zcount = count // group
    nb = NB // group
    top_bit = count.bit_length() - 2
    nblocks = tokens // BLK
    rows_gu = gate_up.shape[0]
    rows_dn = down.shape[0]
    fb = gate_up.shape[3]
    size_gu = rows_gu * 2 * nb * fb

    gu_l = jnp.transpose(gate_up.reshape(rows_gu, 2, group, nb, fb), (2, 0, 1, 3, 4)).reshape(group, -1)
    dn_l = jnp.transpose(down.reshape(rows_dn, group, nb, DB), (1, 0, 2, 3)).reshape(group, -1)
    wbuf = jnp.concatenate([gu_l, dn_l], axis=1)
    wbuf = jnp.broadcast_to(wbuf[None], (zcount,) + wbuf.shape).reshape(count, -1)
    wrecv = exchange(wbuf)
    w_gu = wrecv[:, :size_gu].reshape(count * rows_gu, 2, nb, fb)
    w_dn = wrecv[:, size_gu:].reshape(count * rows_dn, nb, DB)

    def to_group(field):
        x = field.reshape(tokens, group, nb, DB)
        x = jnp.transpose(x, (1, 0, 2, 3))
        return exchange(x, "loc").reshape(group * tokens, nb, DB)

    def from_group(x):
        x = exchange(x.reshape(group, tokens, nb, DB), "loc")
        return jnp.transpose(x, (1, 0, 2, 3)).reshape(tokens, width)

    grad_out = cotangent[0]
    cot_blk = to_group(grad_out)

    xb = seq_in.reshape(nblocks, BLK, width)
    xb_peer = from_partner(xb, SEQ, top_bit)
    mixed = jnp.einsum("ij,kjd->kid", block_mix, xb, precision=HIGH).reshape(tokens, width)
    mixed_peer = jnp.einsum("ij,kjd->kid", block_mix, xb_peer, precision=HIGH).reshape(tokens, width)
    own_hi = twist_hi[side_of(top_bit)]
    first = own_hi[0] * mixed + own_hi[1] * mixed_peer
    second, first_peer = forward_section(first, twist_lo, 0)
    resid = seq_in + second
    scale = lax.rsqrt(jnp.mean(resid * resid, axis=-1, keepdims=True) + EPS)
    unit = resid * scale
    normed = unit * gain
    x_blk = to_group(normed)

    gate_val = jnp.einsum("tnd,dnf->tnf", x_blk, w_gu[:, 0], precision=HIGH)
    up_val = jnp.einsum("tnd,dnf->tnf", x_blk, w_gu[:, 1], precision=HIGH)
    sig = jax.nn.sigmoid(gate_val)
    act = gate_val * sig
    hidden = act * up_val
    grad_hidden = jnp.einsum("tnd,fnd->tnf", cot_blk, w_dn, precision=HIGH)
    grad_gate = grad_hidden * up_val * sig * (1.0 + gate_val * (1.0 - sig))
    grad_up = grad_hidden * act
    grad_x = jnp.einsum("tnf,dnf->tnd", grad_gate, w_gu[:, 0], precision=HIGH) + jnp.einsum(
        "tnf,dnf->tnd", grad_up, w_gu[:, 1], precision=HIGH
    )
    grad_normed = from_group(grad_x)

    d_gate = jnp.einsum("tnd,tnf->dnf", x_blk, grad_gate, precision=HIGH)
    d_up = jnp.einsum("tnd,tnf->dnf", x_blk, grad_up, precision=HIGH)
    d_gu = jnp.stack([d_gate, d_up], axis=1).reshape(count, -1)
    d_dn = jnp.einsum("tnf,tnd->fnd", hidden, cot_blk, precision=HIGH).reshape(count, -1)
    grecv = exchange(jnp.concatenate([d_gu, d_dn], axis=1))
    grecv = grecv.reshape(zcount, group, -1).sum(axis=0)
    part_gu = jnp.transpose(grecv[:, :size_gu].reshape(group, rows_gu, 2, nb, fb), (1, 2, 0, 3, 4))
    part_gu = part_gu.reshape(rows_gu, 2, NB, fb)
    part_down = jnp.transpose(grecv[:, size_gu:].reshape(group, rows_dn, nb, DB), (1, 0, 2, 3))
    part_down = part_down.reshape(rows_dn, NB, DB)
    n_gu = part_gu.size
    wsum = psum_doubling(jnp.concatenate([part_gu.reshape(-1), part_down.reshape(-1)]), "dp")

    grad_gain_local = jnp.sum(grad_normed * unit, axis=0)
    weighted = grad_normed * gain
    inner = jnp.mean(weighted * resid, axis=-1, keepdims=True)
    grad_resid = grad_out + scale * weighted - resid * scale * scale * scale * inner
    grad_first, term_lo = backward_section(grad_resid, first, first_peer, twist_lo, 0)
    _, term_hi = backward_section(grad_first, mixed, mixed_peer, twist_hi, top_bit)
    far_send, wsum = lax.optimization_barrier((own_hi[1] * grad_first, wsum))
    far_recv = from_partner(far_send, SEQ, top_bit)
    grad_mixed = own_hi[0] * grad_first + far_recv
    grad_mb = grad_mixed.reshape(nblocks, BLK, width)
    keep = (own_hi[0] * grad_first).reshape(nblocks, BLK, width)
    give = (own_hi[1] * grad_first).reshape(nblocks, BLK, width)
    term_block = jnp.einsum("kid,kjd->ij", keep, xb, precision=HIGH) + jnp.einsum(
        "kid,kjd->ij", give, xb_peer, precision=HIGH
    )
    grad_seq = jnp.einsum("ij,kid->kjd", block_mix, grad_mb, precision=HIGH).reshape(tokens, width)
    grad_seq = grad_seq + grad_resid
    smalls = (term_block, term_hi, term_lo, grad_gain_local)
    sbuf = jnp.concatenate([t.reshape(-1) for t in smalls])
    z_bits = [("dp", 0)] + [(SEQ, b) for b in range(group.bit_length() - 1, count.bit_length() - 1)]
    off_z = [(SEQ, b) for b in range(group.bit_length() - 1)]
    off_z += [("dp", b) for b in range(1, lax.axis_size("dp").bit_length() - 1)]
    sfull = sbuf
    for axis, bit in off_z:
        sfull = sfull + from_partner(sfull, axis, bit)
    sfull, far_recv = lax.optimization_barrier((sfull, far_recv))
    for axis, bit in z_bits:
        sfull = sfull + from_partner(sfull, axis, bit)
    sums = []
    at = 0
    for t in smalls:
        sums.append(sfull[at : at + t.size].reshape(t.shape))
        at += t.size
    sum_block, sum_hi, sum_lo, sum_gain = sums
    factor = 1.0 / math.sqrt(lax.axis_size("dp") * count * tokens)
    part_gu = wsum[:n_gu].reshape(part_gu.shape)
    part_down = wsum[n_gu:].reshape(part_down.shape)
    return (
        grad_seq[None],
        part_gu * factor,
        part_down * factor,
        sum_block * factor,
        sum_hi * factor,
        sum_lo * factor,
        sum_gain * factor,
    )


def solution(mesh):
    dp_size, seq_size = mesh.devices.shape
    group = min(seq_size, NB // 2)
    split = Mesh(mesh.devices.reshape(dp_size, seq_size // group, group), ("dp",) + SEQ)
    return jax.shard_map(
        per_device,
        mesh=split,
        in_specs=(
            P("dp", SEQ, None),
            P("dp", SEQ, None),
            P(),
            P(),
            P(),
            P(),
            P(SEQ, None, None, None),
            P(SEQ, None, None),
        ),
        out_specs=(
            P("dp", SEQ, None),
            P(SEQ, None, None, None),
            P(SEQ, None, None),
            P(),
            P(),
            P(),
            P(),
        ),
        check_vma=False,
    )
```

```python
import math

import jax
import jax.numpy as jnp
from jax import lax
from jax.sharding import Mesh, PartitionSpec as P

NB = 16
BLK = 128
DB = 128


HIGH = lax.Precision.HIGHEST
EPS = 1e-05


def axis_count(axis):
    if isinstance(axis, tuple):
        return math.prod(lax.axis_size(a) for a in axis)
    return lax.axis_size(axis)


def from_partner(block, axis, distance):
    count = axis_count(axis)
    route = []
    for low in range(count):
        high = low | 1 << distance
        if high != low and high < count:
            route += [(low, high), (high, low)]
    return lax.ppermute(block, axis, route)


SEQ = ("zh", "loc")


def side_of(bit):
    return lax.axis_index(SEQ) // (1 << bit) % 2


def forward_section(field, coeff, bit):
    partner = from_partner(field, SEQ, bit)
    own = coeff[side_of(bit)]
    return (own[0] * field + own[1] * partner, partner)


def backward_section(grad, field, partner, coeff, bit):
    side = side_of(bit)
    own = coeff[side]
    sent = from_partner(own[1] * grad, SEQ, bit)
    back = own[0] * grad + sent
    term = jnp.stack([jnp.sum(grad * field, axis=0), jnp.sum(grad * partner, axis=0)])
    pick = (jnp.arange(2) == side).astype(jnp.float32)
    return (back, pick[:, None, None] * term[None])


def psum_doubling(x, axis):
    for bit in range(axis_count(axis).bit_length() - 1):
        x = x + from_partner(x, axis, bit)
    return x


def exchange(x, axis=SEQ):
    return lax.all_to_all(x, axis, 0, 0, tiled=True)


def per_device(inputs, cotangent, block_mix, twist_hi, twist_lo, gain, gate_up, down):
    seq_in = inputs[0]
    tokens, width = seq_in.shape
    count = axis_count(SEQ)
    group = lax.axis_size("loc")
    zcount = count // group
    nb = NB // group
    top_bit = count.bit_length() - 2
    nblocks = tokens // BLK
    rows_gu = gate_up.shape[0]
    rows_dn = down.shape[0]
    fb = gate_up.shape[3]
    size_gu = rows_gu * 2 * nb * fb

    gu_l = jnp.transpose(gate_up.reshape(rows_gu, 2, group, nb, fb), (2, 0, 1, 3, 4)).reshape(group, -1)
    dn_l = jnp.transpose(down.reshape(rows_dn, group, nb, DB), (1, 0, 2, 3)).reshape(group, -1)
    wbuf = jnp.concatenate([gu_l, dn_l], axis=1)
    wbuf = jnp.broadcast_to(wbuf[None], (zcount,) + wbuf.shape).reshape(count, -1)

    def to_group(field):
        x = field.reshape(tokens, group, nb, DB)
        x = jnp.transpose(x, (1, 0, 2, 3))
        return exchange(x, "loc").reshape(group * tokens, nb, DB)

    def from_group(x):
        x = exchange(x.reshape(group, tokens, nb, DB), "loc")
        return jnp.transpose(x, (1, 0, 2, 3)).reshape(tokens, width)

    grad_out = cotangent[0]
    cot_blk = to_group(grad_out)
    wbuf, cot_blk = lax.optimization_barrier((wbuf, cot_blk))
    wrecv = exchange(wbuf)
    w_gu = wrecv[:, :size_gu].reshape(count * rows_gu, 2, nb, fb)
    w_dn = wrecv[:, size_gu:].reshape(count * rows_dn, nb, DB)

    xb = seq_in.reshape(nblocks, BLK, width)
    xb_peer = from_partner(xb, SEQ, top_bit)
    mixed = jnp.einsum("ij,kjd->kid", block_mix, xb, precision=HIGH).reshape(tokens, width)
    mixed_peer = jnp.einsum("ij,kjd->kid", block_mix, xb_peer, precision=HIGH).reshape(tokens, width)
    own_hi = twist_hi[side_of(top_bit)]
    first = own_hi[0] * mixed + own_hi[1] * mixed_peer
    second, first_peer = forward_section(first, twist_lo, 0)
    resid = seq_in + second
    scale = lax.rsqrt(jnp.mean(resid * resid, axis=-1, keepdims=True) + EPS)
    unit = resid * scale
    normed = unit * gain
    x_blk = to_group(normed)

    gate_val = jnp.einsum("tnd,dnf->tnf", x_blk, w_gu[:, 0], precision=HIGH)
    up_val = jnp.einsum("tnd,dnf->tnf", x_blk, w_gu[:, 1], precision=HIGH)
    sig = jax.nn.sigmoid(gate_val)
    act = gate_val * sig
    hidden = act * up_val
    grad_hidden = jnp.einsum("tnd,fnd->tnf", cot_blk, w_dn, precision=HIGH)
    grad_gate = grad_hidden * up_val * sig * (1.0 + gate_val * (1.0 - sig))
    grad_up = grad_hidden * act
    grad_x = jnp.einsum("tnf,dnf->tnd", grad_gate, w_gu[:, 0], precision=HIGH) + jnp.einsum(
        "tnf,dnf->tnd", grad_up, w_gu[:, 1], precision=HIGH
    )
    grad_normed = from_group(grad_x)

    d_gate = jnp.einsum("tnd,tnf->dnf", x_blk, grad_gate, precision=HIGH)
    d_up = jnp.einsum("tnd,tnf->dnf", x_blk, grad_up, precision=HIGH)
    d_gu = jnp.stack([d_gate, d_up], axis=1).reshape(count, -1)
    d_dn = jnp.einsum("tnf,tnd->fnd", hidden, cot_blk, precision=HIGH).reshape(count, -1)
    grecv = exchange(jnp.concatenate([d_gu, d_dn], axis=1))
    grecv = grecv.reshape(zcount, group, -1).sum(axis=0)
    part_gu = jnp.transpose(grecv[:, :size_gu].reshape(group, rows_gu, 2, nb, fb), (1, 2, 0, 3, 4))
    part_gu = part_gu.reshape(rows_gu, 2, NB, fb)
    part_down = jnp.transpose(grecv[:, size_gu:].reshape(group, rows_dn, nb, DB), (1, 0, 2, 3))
    part_down = part_down.reshape(rows_dn, NB, DB)
    n_gu = part_gu.size
    wsum = psum_doubling(jnp.concatenate([part_gu.reshape(-1), part_down.reshape(-1)]), "dp")
    part_gu = wsum[:n_gu].reshape(part_gu.shape)
    part_down = wsum[n_gu:].reshape(part_down.shape)

    grad_gain_local = jnp.sum(grad_normed * unit, axis=0)
    weighted = grad_normed * gain
    inner = jnp.mean(weighted * resid, axis=-1, keepdims=True)
    grad_resid = grad_out + scale * weighted - resid * scale * scale * scale * inner
    grad_first, term_lo = backward_section(grad_resid, first, first_peer, twist_lo, 0)
    grad_mixed, term_hi = backward_section(grad_first, mixed, mixed_peer, twist_hi, top_bit)
    grad_mb = grad_mixed.reshape(nblocks, BLK, width)
    keep = (own_hi[0] * grad_first).reshape(nblocks, BLK, width)
    give = (own_hi[1] * grad_first).reshape(nblocks, BLK, width)
    term_block = jnp.einsum("kid,kjd->ij", keep, xb, precision=HIGH) + jnp.einsum(
        "kid,kjd->ij", give, xb_peer, precision=HIGH
    )
    grad_seq = jnp.einsum("ij,kid->kjd", block_mix, grad_mb, precision=HIGH).reshape(tokens, width)
    grad_seq = grad_seq + grad_resid
    smalls = (term_block, term_hi, term_lo, grad_gain_local)
    sbuf = jnp.concatenate([t.reshape(-1) for t in smalls])
    spart = exchange(sbuf.reshape(count, -1)).sum(axis=0)
    spart = psum_doubling(spart, "dp")
    sfull = exchange(jnp.broadcast_to(spart[None], (count, spart.shape[0]))).reshape(-1)
    sums = []
    at = 0
    for t in smalls:
        sums.append(sfull[at : at + t.size].reshape(t.shape))
        at += t.size
    sum_block, sum_hi, sum_lo, sum_gain = sums
    factor = 1.0 / math.sqrt(lax.axis_size("dp") * count * tokens)
    return (
        grad_seq[None],
        part_gu * factor,
        part_down * factor,
        sum_block * factor,
        sum_hi * factor,
        sum_lo * factor,
        sum_gain * factor,
    )


def solution(mesh):
    dp_size, seq_size = mesh.devices.shape
    group = min(seq_size, NB // 2)
    split = Mesh(mesh.devices.reshape(dp_size, seq_size // group, group), ("dp",) + SEQ)
    return jax.shard_map(
        per_device,
        mesh=split,
        in_specs=(
            P("dp", SEQ, None),
            P("dp", SEQ, None),
            P(),
            P(),
            P(),
            P(),
            P(SEQ, None, None, None),
            P(SEQ, None, None),
        ),
        out_specs=(
            P("dp", SEQ, None),
            P(SEQ, None, None, None),
            P(SEQ, None, None),
            P(),
            P(),
            P(),
            P(),
        ),
        check_vma=False,
    )
```

```python
import math

import jax
import jax.numpy as jnp
from jax import lax
from jax.sharding import Mesh, PartitionSpec as P

NB = 16
BLK = 128
DB = 128


HIGH = lax.Precision.HIGHEST
EPS = 1e-05


def axis_count(axis):
    if isinstance(axis, tuple):
        return math.prod(lax.axis_size(a) for a in axis)
    return lax.axis_size(axis)


def from_partner(block, axis, distance):
    count = axis_count(axis)
    route = []
    for low in range(count):
        high = low | 1 << distance
        if high != low and high < count:
            route += [(low, high), (high, low)]
    return lax.ppermute(block, axis, route)


SEQ = ("zh", "loc")


def side_of(bit):
    return lax.axis_index(SEQ) // (1 << bit) % 2


def forward_section(field, coeff, bit):
    partner = from_partner(field, SEQ, bit)
    own = coeff[side_of(bit)]
    return (own[0] * field + own[1] * partner, partner)


def backward_section(grad, field, partner, coeff, bit):
    side = side_of(bit)
    own = coeff[side]
    sent = from_partner(own[1] * grad, SEQ, bit)
    back = own[0] * grad + sent
    term = jnp.stack([jnp.sum(grad * field, axis=0), jnp.sum(grad * partner, axis=0)])
    pick = (jnp.arange(2) == side).astype(jnp.float32)
    return (back, pick[:, None, None] * term[None])


def psum_doubling(x, axis):
    for bit in range(axis_count(axis).bit_length() - 1):
        x = x + from_partner(x, axis, bit)
    return x


def exchange(x, axis=SEQ):
    return lax.all_to_all(x, axis, 0, 0, tiled=True)


def per_device(inputs, cotangent, block_mix, twist_hi, twist_lo, gain, gate_up, down):
    seq_in = inputs[0]
    tokens, width = seq_in.shape
    count = axis_count(SEQ)
    group = lax.axis_size("loc")
    zcount = count // group
    nb = NB // group
    top_bit = count.bit_length() - 2
    nblocks = tokens // BLK
    rows_gu = gate_up.shape[0]
    rows_dn = down.shape[0]
    fb = gate_up.shape[3]
    size_gu = rows_gu * 2 * nb * fb

    gu_l = jnp.transpose(gate_up.reshape(rows_gu, 2, group, nb, fb), (2, 0, 1, 3, 4)).reshape(group, -1)
    dn_l = jnp.transpose(down.reshape(rows_dn, group, nb, DB), (1, 0, 2, 3)).reshape(group, -1)
    wbuf = jnp.concatenate([gu_l, dn_l], axis=1)
    wbuf = jnp.broadcast_to(wbuf[None], (zcount,) + wbuf.shape).reshape(count, -1)
    wrecv = exchange(wbuf)
    w_gu = wrecv[:, :size_gu].reshape(count * rows_gu, 2, nb, fb)
    w_dn = wrecv[:, size_gu:].reshape(count * rows_dn, nb, DB)

    def to_group(field):
        x = field.reshape(tokens, group, nb, DB)
        x = jnp.transpose(x, (1, 0, 2, 3))
        return exchange(x, "loc").reshape(group * tokens, nb, DB)

    def from_group(x):
        x = exchange(x.reshape(group, tokens, nb, DB), "loc")
        return jnp.transpose(x, (1, 0, 2, 3)).reshape(tokens, width)

    grad_out = cotangent[0]
    cot_blk = to_group(grad_out)

    xb = seq_in.reshape(nblocks, BLK, width)
    xb_peer = from_partner(xb, SEQ, top_bit)
    mixed = jnp.einsum("ij,kjd->kid", block_mix, xb, precision=HIGH).reshape(tokens, width)
    mixed_peer = jnp.einsum("ij,kjd->kid", block_mix, xb_peer, precision=HIGH).reshape(tokens, width)
    own_hi = twist_hi[side_of(top_bit)]
    first = own_hi[0] * mixed + own_hi[1] * mixed_peer
    second, first_peer = forward_section(first, twist_lo, 0)
    resid = seq_in + second
    scale = lax.rsqrt(jnp.mean(resid * resid, axis=-1, keepdims=True) + EPS)
    unit = resid * scale
    normed = unit * gain
    x_blk = to_group(normed)

    gate_val = jnp.einsum("tnd,dnf->tnf", x_blk, w_gu[:, 0], precision=HIGH)
    up_val = jnp.einsum("tnd,dnf->tnf", x_blk, w_gu[:, 1], precision=HIGH)
    sig = jax.nn.sigmoid(gate_val)
    act = gate_val * sig
    hidden = act * up_val
    grad_hidden = jnp.einsum("tnd,fnd->tnf", cot_blk, w_dn, precision=HIGH)
    grad_gate = grad_hidden * up_val * sig * (1.0 + gate_val * (1.0 - sig))
    grad_up = grad_hidden * act
    grad_x = jnp.einsum("tnf,dnf->tnd", grad_gate, w_gu[:, 0], precision=HIGH) + jnp.einsum(
        "tnf,dnf->tnd", grad_up, w_gu[:, 1], precision=HIGH
    )
    grad_normed = from_group(grad_x)

    d_gate = jnp.einsum("tnd,tnf->dnf", x_blk, grad_gate, precision=HIGH)
    d_up = jnp.einsum("tnd,tnf->dnf", x_blk, grad_up, precision=HIGH)
    d_gu = jnp.stack([d_gate, d_up], axis=1).reshape(count, -1)
    d_dn = jnp.einsum("tnf,tnd->fnd", hidden, cot_blk, precision=HIGH).reshape(count, -1)
    acc = jnp.concatenate([d_gu, d_dn], axis=1).reshape(zcount, group, -1)
    for bit in range(count.bit_length() - 2, group.bit_length() - 2, -1):
        acc = acc.reshape(2, -1, group, acc.shape[-1])
        mine = side_of(bit)
        keep = lax.dynamic_index_in_dim(acc, mine, 0, keepdims=False)
        send = lax.dynamic_index_in_dim(acc, 1 - mine, 0, keepdims=False)
        acc = keep + from_partner(send, SEQ, bit)
    acc, grad_normed = lax.optimization_barrier((acc, grad_normed))
    grecv = exchange(acc.reshape(group, -1), "loc")
    part_gu = jnp.transpose(grecv[:, :size_gu].reshape(group, rows_gu, 2, nb, fb), (1, 2, 0, 3, 4))
    part_gu = part_gu.reshape(rows_gu, 2, NB, fb)
    part_down = jnp.transpose(grecv[:, size_gu:].reshape(group, rows_dn, nb, DB), (1, 0, 2, 3))
    part_down = part_down.reshape(rows_dn, NB, DB)
    n_gu = part_gu.size
    wsum = psum_doubling(jnp.concatenate([part_gu.reshape(-1), part_down.reshape(-1)]), "dp")
    part_gu = wsum[:n_gu].reshape(part_gu.shape)
    part_down = wsum[n_gu:].reshape(part_down.shape)

    grad_gain_local = jnp.sum(grad_normed * unit, axis=0)
    weighted = grad_normed * gain
    inner = jnp.mean(weighted * resid, axis=-1, keepdims=True)
    grad_resid = grad_out + scale * weighted - resid * scale * scale * scale * inner
    grad_first, term_lo = backward_section(grad_resid, first, first_peer, twist_lo, 0)
    grad_mixed, term_hi = backward_section(grad_first, mixed, mixed_peer, twist_hi, top_bit)
    grad_mb = grad_mixed.reshape(nblocks, BLK, width)
    keep = (own_hi[0] * grad_first).reshape(nblocks, BLK, width)
    give = (own_hi[1] * grad_first).reshape(nblocks, BLK, width)
    term_block = jnp.einsum("kid,kjd->ij", keep, xb, precision=HIGH) + jnp.einsum(
        "kid,kjd->ij", give, xb_peer, precision=HIGH
    )
    grad_seq = jnp.einsum("ij,kid->kjd", block_mix, grad_mb, precision=HIGH).reshape(tokens, width)
    grad_seq = grad_seq + grad_resid
    smalls = (term_block, term_hi, term_lo, grad_gain_local)
    sbuf = jnp.concatenate([t.reshape(-1) for t in smalls])
    spart = exchange(sbuf.reshape(count, -1)).sum(axis=0)
    spart = psum_doubling(spart, "dp")
    sfull = exchange(jnp.broadcast_to(spart[None], (count, spart.shape[0]))).reshape(-1)
    sums = []
    at = 0
    for t in smalls:
        sums.append(sfull[at : at + t.size].reshape(t.shape))
        at += t.size
    sum_block, sum_hi, sum_lo, sum_gain = sums
    factor = 1.0 / math.sqrt(lax.axis_size("dp") * count * tokens)
    return (
        grad_seq[None],
        part_gu * factor,
        part_down * factor,
        sum_block * factor,
        sum_hi * factor,
        sum_lo * factor,
        sum_gain * factor,
    )


def solution(mesh):
    dp_size, seq_size = mesh.devices.shape
    group = min(seq_size, NB // 2)
    split = Mesh(mesh.devices.reshape(dp_size, seq_size // group, group), ("dp",) + SEQ)
    return jax.shard_map(
        per_device,
        mesh=split,
        in_specs=(
            P("dp", SEQ, None),
            P("dp", SEQ, None),
            P(),
            P(),
            P(),
            P(),
            P(SEQ, None, None, None),
            P(SEQ, None, None),
        ),
        out_specs=(
            P("dp", SEQ, None),
            P(SEQ, None, None, None),
            P(SEQ, None, None),
            P(),
            P(),
            P(),
            P(),
        ),
        check_vma=False,
    )
```

```python
import math

import jax
import jax.numpy as jnp
from jax import lax
from jax.sharding import Mesh, PartitionSpec as P

NB = 16
BLK = 128
DB = 128


HIGH = lax.Precision.HIGHEST
EPS = 1e-05


def axis_count(axis):
    if isinstance(axis, tuple):
        return math.prod(lax.axis_size(a) for a in axis)
    return lax.axis_size(axis)


def from_partner(block, axis, distance):
    count = axis_count(axis)
    route = []
    for low in range(count):
        high = low | 1 << distance
        if high != low and high < count:
            route += [(low, high), (high, low)]
    return lax.ppermute(block, axis, route)


SEQ = ("zh", "loc")


def side_of(bit):
    return lax.axis_index(SEQ) // (1 << bit) % 2


def forward_section(field, coeff, bit):
    partner = from_partner(field, SEQ, bit)
    own = coeff[side_of(bit)]
    return (own[0] * field + own[1] * partner, partner)


def backward_section(grad, field, partner, coeff, bit):
    side = side_of(bit)
    own = coeff[side]
    sent = from_partner(own[1] * grad, SEQ, bit)
    back = own[0] * grad + sent
    term = jnp.stack([jnp.sum(grad * field, axis=0), jnp.sum(grad * partner, axis=0)])
    pick = (jnp.arange(2) == side).astype(jnp.float32)
    return (back, pick[:, None, None] * term[None])


def psum_doubling(x, axis):
    for bit in range(axis_count(axis).bit_length() - 1):
        x = x + from_partner(x, axis, bit)
    return x


def exchange(x, axis=SEQ):
    return lax.all_to_all(x, axis, 0, 0, tiled=True)


def per_device(inputs, cotangent, block_mix, twist_hi, twist_lo, gain, gate_up, down):
    seq_in = inputs[0]
    tokens, width = seq_in.shape
    count = axis_count(SEQ)
    group = lax.axis_size("loc")
    zcount = count // group
    nb = NB // group
    top_bit = count.bit_length() - 2
    nblocks = tokens // BLK
    rows_gu = gate_up.shape[0]
    rows_dn = down.shape[0]
    fb = gate_up.shape[3]
    size_gu = rows_gu * 2 * nb * fb

    gu_l = jnp.transpose(gate_up.reshape(rows_gu, 2, group, nb, fb), (2, 0, 1, 3, 4)).reshape(group, -1)
    dn_l = jnp.transpose(down.reshape(rows_dn, group, nb, DB), (1, 0, 2, 3)).reshape(group, -1)
    wbuf = jnp.concatenate([gu_l, dn_l], axis=1)
    wbuf = jnp.broadcast_to(wbuf[None], (zcount,) + wbuf.shape).reshape(count, -1)
    wrecv = exchange(wbuf)
    w_gu = wrecv[:, :size_gu].reshape(count * rows_gu, 2, nb, fb)
    w_dn = wrecv[:, size_gu:].reshape(count * rows_dn, nb, DB)

    def to_group(field):
        x = field.reshape(tokens, group, nb, DB)
        x = jnp.transpose(x, (1, 0, 2, 3))
        return exchange(x, "loc").reshape(group * tokens, nb, DB)

    def from_group(x):
        x = exchange(x.reshape(group, tokens, nb, DB), "loc")
        return jnp.transpose(x, (1, 0, 2, 3)).reshape(tokens, width)

    grad_out = cotangent[0]
    cot_blk = to_group(grad_out)

    xb = seq_in.reshape(nblocks, BLK, width)
    xb_peer = from_partner(xb, SEQ, top_bit)
    mixed = jnp.einsum("ij,kjd->kid", block_mix, xb, precision=HIGH).reshape(tokens, width)
    mixed_peer = jnp.einsum("ij,kjd->kid", block_mix, xb_peer, precision=HIGH).reshape(tokens, width)
    own_hi = twist_hi[side_of(top_bit)]
    first = own_hi[0] * mixed + own_hi[1] * mixed_peer
    second, first_peer = forward_section(first, twist_lo, 0)
    resid = seq_in + second
    scale = lax.rsqrt(jnp.mean(resid * resid, axis=-1, keepdims=True) + EPS)
    unit = resid * scale
    normed = unit * gain
    x_blk = to_group(normed)

    gate_val = jnp.einsum("tnd,dnf->tnf", x_blk, w_gu[:, 0], precision=HIGH)
    up_val = jnp.einsum("tnd,dnf->tnf", x_blk, w_gu[:, 1], precision=HIGH)
    sig = jax.nn.sigmoid(gate_val)
    act = gate_val * sig
    hidden = act * up_val
    grad_hidden = jnp.einsum("tnd,fnd->tnf", cot_blk, w_dn, precision=HIGH)
    grad_gate = grad_hidden * up_val * sig * (1.0 + gate_val * (1.0 - sig))
    grad_up = grad_hidden * act
    grad_x = jnp.einsum("tnf,dnf->tnd", grad_gate, w_gu[:, 0], precision=HIGH) + jnp.einsum(
        "tnf,dnf->tnd", grad_up, w_gu[:, 1], precision=HIGH
    )
    grad_normed = from_group(grad_x)

    d_gate = jnp.einsum("tnd,tnf->dnf", x_blk, grad_gate, precision=HIGH)
    d_up = jnp.einsum("tnd,tnf->dnf", x_blk, grad_up, precision=HIGH)
    d_gu = jnp.stack([d_gate, d_up], axis=1).reshape(count, -1)
    d_dn = jnp.einsum("tnf,tnd->fnd", hidden, cot_blk, precision=HIGH).reshape(count, -1)
    wsend = jnp.concatenate([d_gu, d_dn], axis=1)
    grad_gain_local = jnp.sum(grad_normed * unit, axis=0)
    weighted = grad_normed * gain
    inner = jnp.mean(weighted * resid, axis=-1, keepdims=True)
    grad_resid = grad_out + scale * weighted - resid * scale * scale * scale * inner
    grad_first, term_lo = backward_section(grad_resid, first, first_peer, twist_lo, 0)
    wsend, grad_first = lax.optimization_barrier((wsend, grad_first))
    grecv = exchange(wsend)
    grecv = grecv.reshape(zcount, group, -1).sum(axis=0)
    part_gu = jnp.transpose(grecv[:, :size_gu].reshape(group, rows_gu, 2, nb, fb), (1, 2, 0, 3, 4))
    part_gu = part_gu.reshape(rows_gu, 2, NB, fb)
    part_down = jnp.transpose(grecv[:, size_gu:].reshape(group, rows_dn, nb, DB), (1, 0, 2, 3))
    part_down = part_down.reshape(rows_dn, NB, DB)
    n_gu = part_gu.size
    wsum = psum_doubling(jnp.concatenate([part_gu.reshape(-1), part_down.reshape(-1)]), "dp")
    part_gu = wsum[:n_gu].reshape(part_gu.shape)
    part_down = wsum[n_gu:].reshape(part_down.shape)

    grad_mixed, term_hi = backward_section(grad_first, mixed, mixed_peer, twist_hi, top_bit)
    grad_mb = grad_mixed.reshape(nblocks, BLK, width)
    keep = (own_hi[0] * grad_first).reshape(nblocks, BLK, width)
    give = (own_hi[1] * grad_first).reshape(nblocks, BLK, width)
    term_block = jnp.einsum("kid,kjd->ij", keep, xb, precision=HIGH) + jnp.einsum(
        "kid,kjd->ij", give, xb_peer, precision=HIGH
    )
    grad_seq = jnp.einsum("ij,kid->kjd", block_mix, grad_mb, precision=HIGH).reshape(tokens, width)
    grad_seq = grad_seq + grad_resid
    smalls = (term_block, term_hi, term_lo, grad_gain_local)
    sbuf = jnp.concatenate([t.reshape(-1) for t in smalls])
    spart = exchange(sbuf.reshape(count, -1)).sum(axis=0)
    spart = psum_doubling(spart, "dp")
    sfull = exchange(jnp.broadcast_to(spart[None], (count, spart.shape[0]))).reshape(-1)
    sums = []
    at = 0
    for t in smalls:
        sums.append(sfull[at : at + t.size].reshape(t.shape))
        at += t.size
    sum_block, sum_hi, sum_lo, sum_gain = sums
    factor = 1.0 / math.sqrt(lax.axis_size("dp") * count * tokens)
    return (
        grad_seq[None],
        part_gu * factor,
        part_down * factor,
        sum_block * factor,
        sum_hi * factor,
        sum_lo * factor,
        sum_gain * factor,
    )


def solution(mesh):
    dp_size, seq_size = mesh.devices.shape
    group = min(seq_size, NB // 2)
    split = Mesh(mesh.devices.reshape(dp_size, seq_size // group, group), ("dp",) + SEQ)
    return jax.shard_map(
        per_device,
        mesh=split,
        in_specs=(
            P("dp", SEQ, None),
            P("dp", SEQ, None),
            P(),
            P(),
            P(),
            P(),
            P(SEQ, None, None, None),
            P(SEQ, None, None),
        ),
        out_specs=(
            P("dp", SEQ, None),
            P(SEQ, None, None, None),
            P(SEQ, None, None),
            P(),
            P(),
            P(),
            P(),
        ),
        check_vma=False,
    )
```

```python
import math

import jax
import jax.numpy as jnp
from jax import lax
from jax.sharding import Mesh, PartitionSpec as P

NB = 16
BLK = 128
DB = 128


HIGH = lax.Precision.HIGH
EPS = 1e-05


def axis_count(axis):
    if isinstance(axis, tuple):
        return math.prod(lax.axis_size(a) for a in axis)
    return lax.axis_size(axis)


def from_partner(block, axis, distance):
    count = axis_count(axis)
    route = []
    for low in range(count):
        high = low | 1 << distance
        if high != low and high < count:
            route += [(low, high), (high, low)]
    return lax.ppermute(block, axis, route)


SEQ = ("zh", "loc")


def side_of(bit):
    return lax.axis_index(SEQ) // (1 << bit) % 2


def forward_section(field, coeff, bit):
    partner = from_partner(field, SEQ, bit)
    own = coeff[side_of(bit)]
    return (own[0] * field + own[1] * partner, partner)


def backward_section(grad, field, partner, coeff, bit):
    side = side_of(bit)
    own = coeff[side]
    sent = from_partner(own[1] * grad, SEQ, bit)
    back = own[0] * grad + sent
    term = jnp.stack([jnp.sum(grad * field, axis=0), jnp.sum(grad * partner, axis=0)])
    pick = (jnp.arange(2) == side).astype(jnp.float32)
    return (back, pick[:, None, None] * term[None])


def psum_doubling(x, axis):
    for bit in range(axis_count(axis).bit_length() - 1):
        x = x + from_partner(x, axis, bit)
    return x


def exchange(x, axis=SEQ):
    return lax.all_to_all(x, axis, 0, 0, tiled=True)


def per_device(inputs, cotangent, block_mix, twist_hi, twist_lo, gain, gate_up, down):
    seq_in = inputs[0]
    tokens, width = seq_in.shape
    count = axis_count(SEQ)
    group = lax.axis_size("loc")
    zcount = count // group
    nb = NB // group
    top_bit = count.bit_length() - 2
    nblocks = tokens // BLK
    rows_gu = gate_up.shape[0]
    rows_dn = down.shape[0]
    fb = gate_up.shape[3]
    size_gu = rows_gu * 2 * nb * fb

    gu_l = jnp.transpose(gate_up.reshape(rows_gu, 2, group, nb, fb), (2, 0, 1, 3, 4)).reshape(group, -1)
    dn_l = jnp.transpose(down.reshape(rows_dn, group, nb, DB), (1, 0, 2, 3)).reshape(group, -1)
    wbuf = jnp.concatenate([gu_l, dn_l], axis=1)
    wbuf = jnp.broadcast_to(wbuf[None], (zcount,) + wbuf.shape).reshape(count, -1)
    wrecv = exchange(wbuf)
    w_gu = wrecv[:, :size_gu].reshape(count * rows_gu, 2, nb, fb)
    w_dn = wrecv[:, size_gu:].reshape(count * rows_dn, nb, DB)

    def to_group(field):
        x = field.reshape(tokens, group, nb, DB)
        x = jnp.transpose(x, (1, 0, 2, 3))
        return exchange(x, "loc").reshape(group * tokens, nb, DB)

    def from_group(x):
        x = exchange(x.reshape(group, tokens, nb, DB), "loc")
        return jnp.transpose(x, (1, 0, 2, 3)).reshape(tokens, width)

    grad_out = cotangent[0]
    cot_blk = to_group(grad_out)

    xb = seq_in.reshape(nblocks, BLK, width)
    xb_peer = from_partner(xb, SEQ, top_bit)
    mixed = jnp.einsum("ij,kjd->kid", block_mix, xb, precision=HIGH).reshape(tokens, width)
    mixed_peer = jnp.einsum("ij,kjd->kid", block_mix, xb_peer, precision=HIGH).reshape(tokens, width)
    own_hi = twist_hi[side_of(top_bit)]
    first = own_hi[0] * mixed + own_hi[1] * mixed_peer
    second, first_peer = forward_section(first, twist_lo, 0)
    resid = seq_in + second
    scale = lax.rsqrt(jnp.mean(resid * resid, axis=-1, keepdims=True) + EPS)
    unit = resid * scale
    normed = unit * gain
    x_blk = to_group(normed)

    gate_val = jnp.einsum("tnd,dnf->tnf", x_blk, w_gu[:, 0], precision=HIGH)
    up_val = jnp.einsum("tnd,dnf->tnf", x_blk, w_gu[:, 1], precision=HIGH)
    sig = jax.nn.sigmoid(gate_val)
    act = gate_val * sig
    hidden = act * up_val
    grad_hidden = jnp.einsum("tnd,fnd->tnf", cot_blk, w_dn, precision=HIGH)
    grad_gate = grad_hidden * up_val * sig * (1.0 + gate_val * (1.0 - sig))
    grad_up = grad_hidden * act
    grad_x = jnp.einsum("tnf,dnf->tnd", grad_gate, w_gu[:, 0], precision=HIGH) + jnp.einsum(
        "tnf,dnf->tnd", grad_up, w_gu[:, 1], precision=HIGH
    )
    grad_normed = from_group(grad_x)

    d_gate = jnp.einsum("tnd,tnf->dnf", x_blk, grad_gate, precision=HIGH)
    d_up = jnp.einsum("tnd,tnf->dnf", x_blk, grad_up, precision=HIGH)
    d_gu = jnp.stack([d_gate, d_up], axis=1).reshape(count, -1)
    d_dn = jnp.einsum("tnf,tnd->fnd", hidden, cot_blk, precision=HIGH).reshape(count, -1)
    grecv = exchange(jnp.concatenate([d_gu, d_dn], axis=1))
    grecv = grecv.reshape(zcount, group, -1).sum(axis=0)
    part_gu = jnp.transpose(grecv[:, :size_gu].reshape(group, rows_gu, 2, nb, fb), (1, 2, 0, 3, 4))
    part_gu = part_gu.reshape(rows_gu, 2, NB, fb)
    part_down = jnp.transpose(grecv[:, size_gu:].reshape(group, rows_dn, nb, DB), (1, 0, 2, 3))
    part_down = part_down.reshape(rows_dn, NB, DB)
    n_gu = part_gu.size
    wsum = psum_doubling(jnp.concatenate([part_gu.reshape(-1), part_down.reshape(-1)]), "dp")
    part_gu = wsum[:n_gu].reshape(part_gu.shape)
    part_down = wsum[n_gu:].reshape(part_down.shape)

    grad_gain_local = jnp.sum(grad_normed * unit, axis=0)
    weighted = grad_normed * gain
    inner = jnp.mean(weighted * resid, axis=-1, keepdims=True)
    grad_resid = grad_out + scale * weighted - resid * scale * scale * scale * inner
    grad_first, term_lo = backward_section(grad_resid, first, first_peer, twist_lo, 0)
    grad_mixed, term_hi = backward_section(grad_first, mixed, mixed_peer, twist_hi, top_bit)
    grad_mb = grad_mixed.reshape(nblocks, BLK, width)
    keep = (own_hi[0] * grad_first).reshape(nblocks, BLK, width)
    give = (own_hi[1] * grad_first).reshape(nblocks, BLK, width)
    term_block = jnp.einsum("kid,kjd->ij", keep, xb, precision=HIGH) + jnp.einsum(
        "kid,kjd->ij", give, xb_peer, precision=HIGH
    )
    grad_seq = jnp.einsum("ij,kid->kjd", block_mix, grad_mb, precision=HIGH).reshape(tokens, width)
    grad_seq = grad_seq + grad_resid
    smalls = (term_block, term_hi, term_lo, grad_gain_local)
    sbuf = jnp.concatenate([t.reshape(-1) for t in smalls])
    spart = exchange(sbuf.reshape(count, -1)).sum(axis=0)
    spart = psum_doubling(spart, "dp")
    sfull = exchange(jnp.broadcast_to(spart[None], (count, spart.shape[0]))).reshape(-1)
    sums = []
    at = 0
    for t in smalls:
        sums.append(sfull[at : at + t.size].reshape(t.shape))
        at += t.size
    sum_block, sum_hi, sum_lo, sum_gain = sums
    factor = 1.0 / math.sqrt(lax.axis_size("dp") * count * tokens)
    return (
        grad_seq[None],
        part_gu * factor,
        part_down * factor,
        sum_block * factor,
        sum_hi * factor,
        sum_lo * factor,
        sum_gain * factor,
    )


def solution(mesh):
    dp_size, seq_size = mesh.devices.shape
    group = min(seq_size, NB // 2)
    split = Mesh(mesh.devices.reshape(dp_size, seq_size // group, group), ("dp",) + SEQ)
    return jax.shard_map(
        per_device,
        mesh=split,
        in_specs=(
            P("dp", SEQ, None),
            P("dp", SEQ, None),
            P(),
            P(),
            P(),
            P(),
            P(SEQ, None, None, None),
            P(SEQ, None, None),
        ),
        out_specs=(
            P("dp", SEQ, None),
            P(SEQ, None, None, None),
            P(SEQ, None, None),
            P(),
            P(),
            P(),
            P(),
        ),
        check_vma=False,
    )
```

```python
import math

import jax
import jax.numpy as jnp
from jax import lax
from jax.sharding import Mesh, PartitionSpec as P

NB = 16
BLK = 128
DB = 128


HIGH = lax.Precision.HIGH
EPS = 1e-05


def axis_count(axis):
    if isinstance(axis, tuple):
        return math.prod(lax.axis_size(a) for a in axis)
    return lax.axis_size(axis)


def from_partner(block, axis, distance):
    count = axis_count(axis)
    route = []
    for low in range(count):
        high = low | 1 << distance
        if high != low and high < count:
            route += [(low, high), (high, low)]
    return lax.ppermute(block, axis, route)


SEQ = ("zh", "loc")


def side_of(bit):
    return lax.axis_index(SEQ) // (1 << bit) % 2


def forward_section(field, coeff, bit):
    partner = from_partner(field, SEQ, bit)
    own = coeff[side_of(bit)]
    return (own[0] * field + own[1] * partner, partner)


def backward_section(grad, field, partner, coeff, bit):
    side = side_of(bit)
    own = coeff[side]
    sent = from_partner(own[1] * grad, SEQ, bit)
    back = own[0] * grad + sent
    term = jnp.stack([jnp.sum(grad * field, axis=0), jnp.sum(grad * partner, axis=0)])
    pick = (jnp.arange(2) == side).astype(jnp.float32)
    return (back, pick[:, None, None] * term[None])


def psum_doubling(x, axis):
    for bit in reversed(range(axis_count(axis).bit_length() - 1)):
        x = x + from_partner(x, axis, bit)
    return x


def exchange(x, axis=SEQ):
    return lax.all_to_all(x, axis, 0, 0, tiled=True)


def per_device(inputs, cotangent, block_mix, twist_hi, twist_lo, gain, gate_up, down):
    seq_in = inputs[0]
    tokens, width = seq_in.shape
    count = axis_count(SEQ)
    group = lax.axis_size("loc")
    zcount = count // group
    nb = NB // group
    top_bit = count.bit_length() - 2
    nblocks = tokens // BLK
    rows_gu = gate_up.shape[0]
    rows_dn = down.shape[0]
    fb = gate_up.shape[3]
    size_gu = rows_gu * 2 * nb * fb

    gu_l = jnp.transpose(gate_up.reshape(rows_gu, 2, group, nb, fb), (2, 0, 1, 3, 4)).reshape(group, -1)
    dn_l = jnp.transpose(down.reshape(rows_dn, group, nb, DB), (1, 0, 2, 3)).reshape(group, -1)
    wbuf = jnp.concatenate([gu_l, dn_l], axis=1)
    wbuf = jnp.broadcast_to(wbuf[None], (zcount,) + wbuf.shape).reshape(count, -1)
    wrecv = exchange(wbuf)
    w_gu = wrecv[:, :size_gu].reshape(count * rows_gu, 2, nb, fb)
    w_dn = wrecv[:, size_gu:].reshape(count * rows_dn, nb, DB)

    def to_group(field):
        x = field.reshape(tokens, group, nb, DB)
        x = jnp.transpose(x, (1, 0, 2, 3))
        return exchange(x, "loc").reshape(group * tokens, nb, DB)

    def from_group(x):
        x = exchange(x.reshape(group, tokens, nb, DB), "loc")
        return jnp.transpose(x, (1, 0, 2, 3)).reshape(tokens, width)

    grad_out = cotangent[0]
    cot_blk = to_group(grad_out)

    xb = seq_in.reshape(nblocks, BLK, width)
    xb_peer = from_partner(xb, SEQ, top_bit)
    mixed = jnp.einsum("ij,kjd->kid", block_mix, xb, precision=HIGH).reshape(tokens, width)
    mixed_peer = jnp.einsum("ij,kjd->kid", block_mix, xb_peer, precision=HIGH).reshape(tokens, width)
    own_hi = twist_hi[side_of(top_bit)]
    first = own_hi[0] * mixed + own_hi[1] * mixed_peer
    second, first_peer = forward_section(first, twist_lo, 0)
    resid = seq_in + second
    scale = lax.rsqrt(jnp.mean(resid * resid, axis=-1, keepdims=True) + EPS)
    unit = resid * scale
    normed = unit * gain
    x_blk = to_group(normed)

    gate_val = jnp.einsum("tnd,dnf->tnf", x_blk, w_gu[:, 0], precision=HIGH)
    up_val = jnp.einsum("tnd,dnf->tnf", x_blk, w_gu[:, 1], precision=HIGH)
    sig = jax.nn.sigmoid(gate_val)
    act = gate_val * sig
    hidden = act * up_val
    grad_hidden = jnp.einsum("tnd,fnd->tnf", cot_blk, w_dn, precision=HIGH)
    grad_gate = grad_hidden * up_val * sig * (1.0 + gate_val * (1.0 - sig))
    grad_up = grad_hidden * act
    grad_x = jnp.einsum("tnf,dnf->tnd", grad_gate, w_gu[:, 0], precision=HIGH) + jnp.einsum(
        "tnf,dnf->tnd", grad_up, w_gu[:, 1], precision=HIGH
    )
    grad_normed = from_group(grad_x)

    d_gate = jnp.einsum("tnd,tnf->dnf", x_blk, grad_gate, precision=HIGH)
    d_up = jnp.einsum("tnd,tnf->dnf", x_blk, grad_up, precision=HIGH)
    d_gu = jnp.stack([d_gate, d_up], axis=1).reshape(count, -1)
    d_dn = jnp.einsum("tnf,tnd->fnd", hidden, cot_blk, precision=HIGH).reshape(count, -1)
    grecv = exchange(jnp.concatenate([d_gu, d_dn], axis=1))
    grecv = grecv.reshape(zcount, group, -1).sum(axis=0)
    part_gu = jnp.transpose(grecv[:, :size_gu].reshape(group, rows_gu, 2, nb, fb), (1, 2, 0, 3, 4))
    part_gu = part_gu.reshape(rows_gu, 2, NB, fb)
    part_down = jnp.transpose(grecv[:, size_gu:].reshape(group, rows_dn, nb, DB), (1, 0, 2, 3))
    part_down = part_down.reshape(rows_dn, NB, DB)
    n_gu = part_gu.size
    wsum = psum_doubling(jnp.concatenate([part_gu.reshape(-1), part_down.reshape(-1)]), "dp")
    part_gu = wsum[:n_gu].reshape(part_gu.shape)
    part_down = wsum[n_gu:].reshape(part_down.shape)

    grad_gain_local = jnp.sum(grad_normed * unit, axis=0)
    weighted = grad_normed * gain
    inner = jnp.mean(weighted * resid, axis=-1, keepdims=True)
    grad_resid = grad_out + scale * weighted - resid * scale * scale * scale * inner
    grad_first, term_lo = backward_section(grad_resid, first, first_peer, twist_lo, 0)
    grad_mixed, term_hi = backward_section(grad_first, mixed, mixed_peer, twist_hi, top_bit)
    grad_mb = grad_mixed.reshape(nblocks, BLK, width)
    keep = (own_hi[0] * grad_first).reshape(nblocks, BLK, width)
    give = (own_hi[1] * grad_first).reshape(nblocks, BLK, width)
    term_block = jnp.einsum("kid,kjd->ij", keep, xb, precision=HIGH) + jnp.einsum(
        "kid,kjd->ij", give, xb_peer, precision=HIGH
    )
    grad_seq = jnp.einsum("ij,kid->kjd", block_mix, grad_mb, precision=HIGH).reshape(tokens, width)
    grad_seq = grad_seq + grad_resid
    smalls = (term_block, term_hi, term_lo, grad_gain_local)
    sbuf = jnp.concatenate([t.reshape(-1) for t in smalls])
    spart = exchange(sbuf.reshape(count, -1)).sum(axis=0)
    spart = psum_doubling(spart, "dp")
    sfull = exchange(jnp.broadcast_to(spart[None], (count, spart.shape[0]))).reshape(-1)
    sums = []
    at = 0
    for t in smalls:
        sums.append(sfull[at : at + t.size].reshape(t.shape))
        at += t.size
    sum_block, sum_hi, sum_lo, sum_gain = sums
    factor = 1.0 / math.sqrt(lax.axis_size("dp") * count * tokens)
    return (
        grad_seq[None],
        part_gu * factor,
        part_down * factor,
        sum_block * factor,
        sum_hi * factor,
        sum_lo * factor,
        sum_gain * factor,
    )


def solution(mesh):
    dp_size, seq_size = mesh.devices.shape
    group = min(seq_size, NB // 2)
    split = Mesh(mesh.devices.reshape(dp_size, seq_size // group, group), ("dp",) + SEQ)
    return jax.shard_map(
        per_device,
        mesh=split,
        in_specs=(
            P("dp", SEQ, None),
            P("dp", SEQ, None),
            P(),
            P(),
            P(),
            P(),
            P(SEQ, None, None, None),
            P(SEQ, None, None),
        ),
        out_specs=(
            P("dp", SEQ, None),
            P(SEQ, None, None, None),
            P(SEQ, None, None),
            P(),
            P(),
            P(),
            P(),
        ),
        check_vma=False,
    )
```

```python
import math

import jax
import jax.numpy as jnp
from jax import lax
from jax.sharding import Mesh, PartitionSpec as P

NB = 16
BLK = 128
DB = 128


HIGH = lax.Precision.HIGH
EPS = 1e-05


def axis_count(axis):
    if isinstance(axis, tuple):
        return math.prod(lax.axis_size(a) for a in axis)
    return lax.axis_size(axis)


def from_partner(block, axis, distance):
    count = axis_count(axis)
    route = []
    for low in range(count):
        high = low | 1 << distance
        if high != low and high < count:
            route += [(low, high), (high, low)]
    return lax.ppermute(block, axis, route)


SEQ = ("zh", "loc")


def side_of(bit):
    return lax.axis_index(SEQ) // (1 << bit) % 2


def forward_section(field, coeff, bit):
    partner = from_partner(field, SEQ, bit)
    own = coeff[side_of(bit)]
    return (own[0] * field + own[1] * partner, partner)


def backward_section(grad, field, partner, coeff, bit):
    side = side_of(bit)
    own = coeff[side]
    sent = from_partner(own[1] * grad, SEQ, bit)
    back = own[0] * grad + sent
    term = jnp.stack([jnp.sum(grad * field, axis=0), jnp.sum(grad * partner, axis=0)])
    pick = (jnp.arange(2) == side).astype(jnp.float32)
    return (back, pick[:, None, None] * term[None])


def psum_doubling(x, axis):
    for bit in range(axis_count(axis).bit_length() - 1):
        x = x + from_partner(x, axis, bit)
    return x


def exchange(x, axis=SEQ):
    return lax.all_to_all(x, axis, 0, 0, tiled=True)


def per_device(inputs, cotangent, block_mix, twist_hi, twist_lo, gain, gate_up, down):
    seq_in = inputs[0]
    tokens, width = seq_in.shape
    count = axis_count(SEQ)
    group = lax.axis_size("loc")
    zcount = count // group
    nb = NB // group
    top_bit = count.bit_length() - 2
    nblocks = tokens // BLK
    rows_gu = gate_up.shape[0]
    rows_dn = down.shape[0]
    fb = gate_up.shape[3]
    size_gu = rows_gu * 2 * nb * fb

    gu_l = jnp.transpose(gate_up.reshape(rows_gu, 2, group, nb, fb), (2, 0, 1, 3, 4)).reshape(group, -1)
    dn_l = jnp.transpose(down.reshape(rows_dn, group, nb, DB), (1, 0, 2, 3)).reshape(group, -1)
    wbuf = jnp.concatenate([gu_l, dn_l], axis=1)
    wbuf = jnp.broadcast_to(wbuf[None], (zcount,) + wbuf.shape).reshape(count, -1)
    wrecv = exchange(wbuf)
    w_gu = wrecv[:, :size_gu].reshape(count * rows_gu, 2, nb, fb)
    w_dn = wrecv[:, size_gu:].reshape(count * rows_dn, nb, DB)

    def to_group(field):
        x = field.reshape(tokens, group, nb, DB)
        x = jnp.transpose(x, (1, 0, 2, 3))
        return exchange(x, "loc").reshape(group * tokens, nb, DB)

    def from_group(x):
        x = exchange(x.reshape(group, tokens, nb, DB), "loc")
        return jnp.transpose(x, (1, 0, 2, 3)).reshape(tokens, width)

    grad_out = cotangent[0]
    cot_blk = to_group(grad_out)

    xb = seq_in.reshape(nblocks, BLK, width)
    xb_peer = from_partner(xb, SEQ, top_bit)
    mixed = jnp.einsum("ij,kjd->kid", block_mix, xb, precision=HIGH).reshape(tokens, width)
    mixed_peer = jnp.einsum("ij,kjd->kid", block_mix, xb_peer, precision=HIGH).reshape(tokens, width)
    own_hi = twist_hi[side_of(top_bit)]
    first = own_hi[0] * mixed + own_hi[1] * mixed_peer
    second, first_peer = forward_section(first, twist_lo, 0)
    resid = seq_in + second
    scale = lax.rsqrt(jnp.mean(resid * resid, axis=-1, keepdims=True) + EPS)
    unit = resid * scale
    normed = unit * gain
    x_blk = to_group(normed)

    both_val = jnp.einsum("tnd,dgnf->gtnf", x_blk, w_gu, precision=HIGH)
    gate_val, up_val = both_val[0], both_val[1]
    sig = jax.nn.sigmoid(gate_val)
    act = gate_val * sig
    hidden = act * up_val
    grad_hidden = jnp.einsum("tnd,fnd->tnf", cot_blk, w_dn, precision=HIGH)
    grad_gate = grad_hidden * up_val * sig * (1.0 + gate_val * (1.0 - sig))
    grad_up = grad_hidden * act
    grad_both = jnp.stack([grad_gate, grad_up])
    grad_x = jnp.einsum("gtnf,dgnf->tnd", grad_both, w_gu, precision=HIGH)
    grad_normed = from_group(grad_x)

    d_gu = jnp.einsum("tnd,gtnf->dgnf", x_blk, grad_both, precision=HIGH).reshape(count, -1)
    d_dn = jnp.einsum("tnf,tnd->fnd", hidden, cot_blk, precision=HIGH).reshape(count, -1)
    grecv = exchange(jnp.concatenate([d_gu, d_dn], axis=1))
    grecv = grecv.reshape(zcount, group, -1).sum(axis=0)
    part_gu = jnp.transpose(grecv[:, :size_gu].reshape(group, rows_gu, 2, nb, fb), (1, 2, 0, 3, 4))
    part_gu = part_gu.reshape(rows_gu, 2, NB, fb)
    part_down = jnp.transpose(grecv[:, size_gu:].reshape(group, rows_dn, nb, DB), (1, 0, 2, 3))
    part_down = part_down.reshape(rows_dn, NB, DB)
    n_gu = part_gu.size
    wsum = psum_doubling(jnp.concatenate([part_gu.reshape(-1), part_down.reshape(-1)]), "dp")
    part_gu = wsum[:n_gu].reshape(part_gu.shape)
    part_down = wsum[n_gu:].reshape(part_down.shape)

    grad_gain_local = jnp.sum(grad_normed * unit, axis=0)
    weighted = grad_normed * gain
    inner = jnp.mean(weighted * resid, axis=-1, keepdims=True)
    grad_resid = grad_out + scale * weighted - resid * scale * scale * scale * inner
    grad_first, term_lo = backward_section(grad_resid, first, first_peer, twist_lo, 0)
    grad_mixed, term_hi = backward_section(grad_first, mixed, mixed_peer, twist_hi, top_bit)
    grad_mb = grad_mixed.reshape(nblocks, BLK, width)
    keep = (own_hi[0] * grad_first).reshape(nblocks, BLK, width)
    give = (own_hi[1] * grad_first).reshape(nblocks, BLK, width)
    term_block = jnp.einsum("kid,kjd->ij", keep, xb, precision=HIGH) + jnp.einsum(
        "kid,kjd->ij", give, xb_peer, precision=HIGH
    )
    grad_seq = jnp.einsum("ij,kid->kjd", block_mix, grad_mb, precision=HIGH).reshape(tokens, width)
    grad_seq = grad_seq + grad_resid
    smalls = (term_block, term_hi, term_lo, grad_gain_local)
    sbuf = jnp.concatenate([t.reshape(-1) for t in smalls])
    spart = exchange(sbuf.reshape(count, -1)).sum(axis=0)
    spart = psum_doubling(spart, "dp")
    sfull = exchange(jnp.broadcast_to(spart[None], (count, spart.shape[0]))).reshape(-1)
    sums = []
    at = 0
    for t in smalls:
        sums.append(sfull[at : at + t.size].reshape(t.shape))
        at += t.size
    sum_block, sum_hi, sum_lo, sum_gain = sums
    factor = 1.0 / math.sqrt(lax.axis_size("dp") * count * tokens)
    return (
        grad_seq[None],
        part_gu * factor,
        part_down * factor,
        sum_block * factor,
        sum_hi * factor,
        sum_lo * factor,
        sum_gain * factor,
    )


def solution(mesh):
    dp_size, seq_size = mesh.devices.shape
    group = min(seq_size, NB // 2)
    split = Mesh(mesh.devices.reshape(dp_size, seq_size // group, group), ("dp",) + SEQ)
    return jax.shard_map(
        per_device,
        mesh=split,
        in_specs=(
            P("dp", SEQ, None),
            P("dp", SEQ, None),
            P(),
            P(),
            P(),
            P(),
            P(SEQ, None, None, None),
            P(SEQ, None, None),
        ),
        out_specs=(
            P("dp", SEQ, None),
            P(SEQ, None, None, None),
            P(SEQ, None, None),
            P(),
            P(),
            P(),
            P(),
        ),
        check_vma=False,
    )
```

```python
import math

import jax
import jax.numpy as jnp
from jax import lax
from jax.sharding import Mesh, PartitionSpec as P

NB = 16
BLK = 128
DB = 128


HIGH = lax.Precision.HIGH
EPS = 1e-05


def axis_count(axis):
    if isinstance(axis, tuple):
        return math.prod(lax.axis_size(a) for a in axis)
    return lax.axis_size(axis)


def from_partner(block, axis, distance):
    count = axis_count(axis)
    route = []
    for low in range(count):
        high = low | 1 << distance
        if high != low and high < count:
            route += [(low, high), (high, low)]
    return lax.ppermute(block, axis, route)


SEQ = ("zh", "loc")


def side_of(bit):
    return lax.axis_index(SEQ) // (1 << bit) % 2


def forward_section(field, coeff, bit):
    partner = from_partner(field, SEQ, bit)
    own = coeff[side_of(bit)]
    return (own[0] * field + own[1] * partner, partner)


def backward_section(grad, field, partner, coeff, bit):
    side = side_of(bit)
    own = coeff[side]
    sent = from_partner(own[1] * grad, SEQ, bit)
    back = own[0] * grad + sent
    term = jnp.stack([jnp.sum(grad * field, axis=0), jnp.sum(grad * partner, axis=0)])
    pick = (jnp.arange(2) == side).astype(jnp.float32)
    return (back, pick[:, None, None] * term[None])


def psum_doubling(x, axis):
    for bit in range(axis_count(axis).bit_length() - 1):
        x = x + from_partner(x, axis, bit)
    return x


def exchange(x, axis=SEQ):
    return lax.all_to_all(x, axis, 0, 0, tiled=True)


def per_device(inputs, cotangent, block_mix, twist_hi, twist_lo, gain, gate_up, down):
    seq_in = inputs[0]
    tokens, width = seq_in.shape
    count = axis_count(SEQ)
    group = lax.axis_size("loc")
    zcount = count // group
    nb = NB // group
    top_bit = count.bit_length() - 2
    nblocks = tokens // BLK
    rows_gu = gate_up.shape[0]
    rows_dn = down.shape[0]
    fb = gate_up.shape[3]
    size_gu = rows_gu * 2 * nb * fb

    gu_l = jnp.transpose(gate_up.reshape(rows_gu, 2, group, nb, fb), (2, 0, 1, 3, 4)).reshape(group, -1)
    dn_l = jnp.transpose(down.reshape(rows_dn, group, nb, DB), (1, 0, 2, 3)).reshape(group, -1)
    wbuf = jnp.concatenate([gu_l, dn_l], axis=1)
    wbuf = jnp.broadcast_to(wbuf[None], (zcount,) + wbuf.shape).reshape(count, -1)
    wrecv = exchange(wbuf)
    w_gu = wrecv[:, :size_gu].reshape(count * rows_gu, 2, nb, fb)
    w_dn = wrecv[:, size_gu:].reshape(count * rows_dn, nb, DB)

    def to_group(field):
        x = field.reshape(tokens, group, nb, DB)
        x = jnp.transpose(x, (1, 0, 2, 3))
        return exchange(x, "loc").reshape(group * tokens, nb, DB)

    def from_group(x):
        x = exchange(x.reshape(group, tokens, nb, DB), "loc")
        return jnp.transpose(x, (1, 0, 2, 3)).reshape(tokens, width)

    grad_out = cotangent[0]
    cot_blk = to_group(grad_out)

    xb = seq_in.reshape(nblocks, BLK, width)
    xb_peer = from_partner(xb, SEQ, top_bit)
    mixed_both = jnp.einsum("ij,kjd->kid", block_mix, jnp.concatenate([xb, xb_peer]), precision=HIGH)
    mixed = mixed_both[:nblocks].reshape(tokens, width)
    mixed_peer = mixed_both[nblocks:].reshape(tokens, width)
    own_hi = twist_hi[side_of(top_bit)]
    first = own_hi[0] * mixed + own_hi[1] * mixed_peer
    second, first_peer = forward_section(first, twist_lo, 0)
    resid = seq_in + second
    scale = lax.rsqrt(jnp.mean(resid * resid, axis=-1, keepdims=True) + EPS)
    unit = resid * scale
    normed = unit * gain
    x_blk = to_group(normed)

    both_val = jnp.einsum("tnd,dgnf->gtnf", x_blk, w_gu, precision=HIGH)
    gate_val, up_val = both_val[0], both_val[1]
    sig = jax.nn.sigmoid(gate_val)
    act = gate_val * sig
    hidden = act * up_val
    grad_hidden = jnp.einsum("tnd,fnd->tnf", cot_blk, w_dn, precision=HIGH)
    grad_gate = grad_hidden * up_val * sig * (1.0 + gate_val * (1.0 - sig))
    grad_up = grad_hidden * act
    grad_both = jnp.stack([grad_gate, grad_up])
    grad_x = jnp.einsum("gtnf,dgnf->tnd", grad_both, w_gu, precision=HIGH)
    grad_normed = from_group(grad_x)

    d_gu = jnp.einsum("tnd,gtnf->dgnf", x_blk, grad_both, precision=HIGH).reshape(count, -1)
    d_dn = jnp.einsum("tnf,tnd->fnd", hidden, cot_blk, precision=HIGH).reshape(count, -1)
    grecv = exchange(jnp.concatenate([d_gu, d_dn], axis=1))
    grecv = grecv.reshape(zcount, group, -1).sum(axis=0)
    part_gu = jnp.transpose(grecv[:, :size_gu].reshape(group, rows_gu, 2, nb, fb), (1, 2, 0, 3, 4))
    part_gu = part_gu.reshape(rows_gu, 2, NB, fb)
    part_down = jnp.transpose(grecv[:, size_gu:].reshape(group, rows_dn, nb, DB), (1, 0, 2, 3))
    part_down = part_down.reshape(rows_dn, NB, DB)
    n_gu = part_gu.size
    wsum = psum_doubling(jnp.concatenate([part_gu.reshape(-1), part_down.reshape(-1)]), "dp")
    part_gu = wsum[:n_gu].reshape(part_gu.shape)
    part_down = wsum[n_gu:].reshape(part_down.shape)

    grad_gain_local = jnp.sum(grad_normed * unit, axis=0)
    weighted = grad_normed * gain
    inner = jnp.mean(weighted * resid, axis=-1, keepdims=True)
    grad_resid = grad_out + scale * weighted - resid * scale * scale * scale * inner
    grad_first, term_lo = backward_section(grad_resid, first, first_peer, twist_lo, 0)
    grad_mixed, term_hi = backward_section(grad_first, mixed, mixed_peer, twist_hi, top_bit)
    grad_mb = grad_mixed.reshape(nblocks, BLK, width)
    keep = (own_hi[0] * grad_first).reshape(nblocks, BLK, width)
    give = (own_hi[1] * grad_first).reshape(nblocks, BLK, width)
    term_block = jnp.einsum(
        "kid,kjd->ij", jnp.concatenate([keep, give]), jnp.concatenate([xb, xb_peer]), precision=HIGH
    )
    grad_seq = jnp.einsum("ij,kid->kjd", block_mix, grad_mb, precision=HIGH).reshape(tokens, width)
    grad_seq = grad_seq + grad_resid
    smalls = (term_block, term_hi, term_lo, grad_gain_local)
    sbuf = jnp.concatenate([t.reshape(-1) for t in smalls])
    spart = exchange(sbuf.reshape(count, -1)).sum(axis=0)
    spart = psum_doubling(spart, "dp")
    sfull = exchange(jnp.broadcast_to(spart[None], (count, spart.shape[0]))).reshape(-1)
    sums = []
    at = 0
    for t in smalls:
        sums.append(sfull[at : at + t.size].reshape(t.shape))
        at += t.size
    sum_block, sum_hi, sum_lo, sum_gain = sums
    factor = 1.0 / math.sqrt(lax.axis_size("dp") * count * tokens)
    return (
        grad_seq[None],
        part_gu * factor,
        part_down * factor,
        sum_block * factor,
        sum_hi * factor,
        sum_lo * factor,
        sum_gain * factor,
    )


def solution(mesh):
    dp_size, seq_size = mesh.devices.shape
    group = min(seq_size, NB // 2)
    split = Mesh(mesh.devices.reshape(dp_size, seq_size // group, group), ("dp",) + SEQ)
    return jax.shard_map(
        per_device,
        mesh=split,
        in_specs=(
            P("dp", SEQ, None),
            P("dp", SEQ, None),
            P(),
            P(),
            P(),
            P(),
            P(SEQ, None, None, None),
            P(SEQ, None, None),
        ),
        out_specs=(
            P("dp", SEQ, None),
            P(SEQ, None, None, None),
            P(SEQ, None, None),
            P(),
            P(),
            P(),
            P(),
        ),
        check_vma=False,
    )
```
